1024 devices in a mesh: blk: 64 (over z, y_lo, core), head: 16 (over y_hi, x).
Axes of the slice: x: 4, y: 8 (y_hi: 4, y_lo: 2; y = y_hi * 2 + y_lo), z: 16, core: 2. Of those that a mesh axis runs over, the one named last changes fastest.
Arguments:
- queries: bfloat16 [65536, 4096], P(('blk', 'head')), may hold values from -60 to 60
- keys: bfloat16 [65536, 4096], P(('blk', 'head')), may hold values from -6.5 to 6.5
- values: bfloat16 [65536, 4096], P(('blk', 'head')), may hold values from -6 to 6
- block_lists: int32 [256, 3], P('blk'), may hold values from 0 to 255, as said below
- block_counts: int32 [256], P('blk'), may hold values from 1 to 3, as said below
Outputs:
- attended: bfloat16 [65536, 4096], P(('blk', 'head'))
The draws below stay inside these ranges and needn't reach their ends.
Inputs may be any that keep to these rules, and one draw needn't show every extreme that they name: `block_lists`: row q holds distinct block indices among q - 2 to q, none below 0, starting with q itself; only its first block_counts[q] entries are used, and the rest repeat q. block_counts[q] is at most min(q + 1, 3); the last block's count is 3.
All inputs are finite; a program needn't handle non-finite values.
Results may differ from the reference program's by a relative error of at most 0.0037.
Values may be sent and summed in bfloat16 or wider, within the bound.
No kernel may reach another device: no remote copies, remote signals or barrier semaphores. Data moves between devices by JAX's collectives and lax.ppermute only.
A program may use at most 32 MiB of HBM per device.

```python
import jax
import jax.numpy as jnp
from jax import lax

HEADS = 32
HDIM = 128
BLOCK = 256
CYCLE = 3
D = 4096
NBLK = 256
FRAMES = 65536


def sparse_pattern(key):
    first_key = jax.random.fold_in(key, 11)
    second_key = jax.random.fold_in(key, 12)
    rows = jnp.arange(NBLK, dtype=jnp.int32)[:, None]
    dist = jnp.arange(CYCLE, dtype=jnp.int32)[None, :]
    raw = jax.random.randint(first_key, (NBLK, CYCLE), 0, 4096, dtype=jnp.int32)
    score = jnp.where(dist == 0, 4096 * CYCLE * 2, raw * CYCLE + dist)
    score = jnp.where(dist <= rows, score, -1)
    order = jnp.argsort(-score, axis=1).astype(jnp.int32)
    drawn = jax.random.randint(second_key, (NBLK,), 1, CYCLE + 1, dtype=jnp.int32)
    counts = jnp.minimum(drawn, rows[:, 0] + 1)
    counts = jnp.where(jnp.arange(NBLK, dtype=jnp.int32) == NBLK - 1, CYCLE, counts).astype(jnp.int32)
    lists = jnp.where(dist < counts[:, None], rows - order, rows).astype(jnp.int32)
    return (lists, counts)


def draw_block_lists(key, part):
    return sparse_pattern(key)[0]


def draw_block_counts(key, part):
    return sparse_pattern(key)[1]


def key_base(key):
    base_key = jax.random.fold_in(key, 21)
    return jnp.clip(jax.random.normal(base_key, (FRAMES, D), jnp.float32), -6.0, 6.0)


def draw_keys(key, part):
    base = key_base(key)
    return base.astype(jnp.bfloat16)


def draw_queries(key, part):
    query_key = jax.random.fold_in(key, 23)
    base = jnp.clip(jax.random.normal(query_key, (FRAMES, D), jnp.float32), -6.0, 6.0)
    return base.astype(jnp.bfloat16)


def steps_of(key, extent, split, least, high):
    gain = 1.0
    for axis_at, parts in split:
        draws = jax.random.uniform(jax.random.fold_in(jax.random.fold_in(key, 6), axis_at), (parts,), jnp.float32, least / len(split), high / len(split))
        gain = gain * jnp.repeat(jnp.exp(draws), extent[axis_at] // parts).reshape((-1,) + (1,) * (len(extent) - 1 - axis_at))
    return gain


def gaussian(rng, shape, deviation, limit, cuts=(), kind=jnp.bfloat16):
    values = deviation * jax.random.normal(rng, shape, jnp.float32)
    if cuts:
        values = values * steps_of(rng, shape, cuts, -0.22, 0.18)
    return jnp.clip(values, -limit, limit).astype(kind)


def setup_inputs(seed: int = 0) -> dict:
    seeds = jax.random.split(jax.random.key(seed), 6)
    queries = draw_queries(jax.random.fold_in(seeds[5], 71), 0)
    keys = draw_keys(jax.random.fold_in(seeds[5], 71), 0)
    values = gaussian(seeds[2], (FRAMES, D), 1.0, 6.0, ((0, 1024),))
    block_lists = draw_block_lists(jax.random.fold_in(seeds[5], 71), 0)
    block_counts = draw_block_counts(jax.random.fold_in(seeds[5], 71), 0)
    return dict(queries=queries, keys=keys, values=values, block_lists=block_lists, block_counts=block_counts)


def reference(queries, keys, values, block_lists, block_counts):
    nblk = FRAMES // BLOCK
    scale = 1.0 / (HDIM ** 0.5)
    qall = queries.reshape(nblk, BLOCK, HEADS, HDIM)
    kall = keys.reshape(nblk, BLOCK, HEADS, HDIM)
    vall = values.reshape(nblk, BLOCK, HEADS, HDIM)

    def one_block(index):
        qblock = lax.dynamic_index_in_dim(qall, index, 0, keepdims=False).astype(jnp.float32)
        picks = lax.dynamic_index_in_dim(block_lists, index, 0, keepdims=False).astype(jnp.int32)
        count = lax.dynamic_index_in_dim(block_counts, index, 0, keepdims=False)
        kblock = kall[picks].reshape(CYCLE * BLOCK, HEADS, HDIM).astype(jnp.float32)
        vblock = vall[picks].reshape(CYCLE * BLOCK, HEADS, HDIM).astype(jnp.float32)
        valid = jnp.arange(CYCLE, dtype=jnp.int32) < count
        key_frame = (picks[:, None] * BLOCK + jnp.arange(BLOCK, dtype=jnp.int32)[None, :]).reshape(-1)
        query_frame = index * BLOCK + jnp.arange(BLOCK, dtype=jnp.int32)
        mask = jnp.repeat(valid, BLOCK)[None, :] & (key_frame[None, :] <= query_frame[:, None])
        scores = jnp.einsum("qhd,khd->hqk", qblock, kblock) * scale
        scores = jnp.where(mask[None], scores, -1e30)
        top = jnp.max(scores, axis=-1, keepdims=True)
        weights = jnp.where(mask[None], jnp.exp(scores - top), 0.0)
        total = jnp.sum(weights, axis=-1)
        rounded = lax.optimization_barrier(weights.astype(jnp.bfloat16)).astype(jnp.float32)
        summed = jnp.einsum("hqk,khd->qhd", rounded, vblock)
        result = summed / jnp.transpose(total)[:, :, None]
        return result.reshape(BLOCK, HEADS * HDIM).astype(jnp.bfloat16)

    blocks = lax.map(one_block, jnp.arange(nblk, dtype=jnp.int32))
    return blocks.reshape(FRAMES, HEADS * HDIM)
```

```python
import jax
import jax.numpy as jnp
from jax import lax
from jax.experimental import pallas as pl
from jax.experimental.pallas import tpu as pltpu
from jax.sharding import PartitionSpec as P

HEADS = 32
HDIM = 128
BLOCK = 256
CYCLE = 3


def from_behind(value, axis, steps):
    count = lax.axis_size(axis)
    initial, last = (max(0, -steps), min(count, count - steps))
    return lax.ppermute(value, axis, [(source, source + steps) for source in range(initial, last)])


def attention_kernel(flags_ref, qkv_ref, before_ref, out_ref):
    rows = qkv_ref.shape[1]
    owned_blocks = rows // BLOCK
    local_heads = qkv_ref.shape[2] // HDIM
    reach = CYCLE - 1
    scale = 1.0 / HDIM**0.5
    row_pos = lax.broadcasted_iota(jnp.int32, (BLOCK, BLOCK), 0)
    col_pos = lax.broadcasted_iota(jnp.int32, (BLOCK, BLOCK), 1)
    causal = col_pos <= row_pos
    for local in range(owned_blocks):
        wanted = [flags_ref[local, place] != 0 for place in range(CYCLE)]
        masks = []
        for place in range(CYCLE):
            if place == reach:
                masks.append(causal & wanted[place])
            else:
                masks.append(jnp.broadcast_to(wanted[place], (BLOCK, BLOCK)))
        for head in range(local_heads):
            cols = slice(head * HDIM, (head + 1) * HDIM)
            q = qkv_ref[0, local * BLOCK : (local + 1) * BLOCK, cols]
            parts = []
            for place in range(CYCLE):
                source = local - (reach - place)
                if source >= 0:
                    k = qkv_ref[1, source * BLOCK : (source + 1) * BLOCK, cols]
                    v = qkv_ref[2, source * BLOCK : (source + 1) * BLOCK, cols]
                else:
                    start = (source + reach) * BLOCK
                    k = before_ref[0, start : start + BLOCK, cols]
                    v = before_ref[1, start : start + BLOCK, cols]
                s = lax.dot_general(q, k, (((1,), (1,)), ((), ())), preferred_element_type=jnp.float32) * scale
                s = jnp.where(masks[place], s, -1e30)
                parts.append((s, v))
            top = jnp.max(parts[0][0], axis=1, keepdims=True)
            for s, _ in parts[1:]:
                top = jnp.maximum(top, jnp.max(s, axis=1, keepdims=True))
            total = None
            summed = None
            for place, (s, v) in enumerate(parts):
                w = jnp.where(masks[place], jnp.exp(s - top), 0.0)
                t = jnp.sum(w, axis=1, keepdims=True)
                o = jnp.dot(w.astype(jnp.bfloat16), v, preferred_element_type=jnp.float32)
                total = t if total is None else total + t
                summed = o if summed is None else summed + o
            out_ref[local * BLOCK : (local + 1) * BLOCK, cols] = (summed / total).astype(out_ref.dtype)


def body(queries, keys, values, block_lists, block_counts):
    qkv = jnp.stack((queries, keys, values))
    mine = lax.all_to_all(qkv, "head", split_axis=2, concat_axis=1, tiled=True)
    rows = mine.shape[1]
    owned_blocks = rows // BLOCK
    reach = CYCLE - 1
    before = from_behind(mine[1:, rows - reach * BLOCK :], "blk", 1)
    own = lax.axis_index("blk")
    target = own * owned_blocks + jnp.arange(owned_blocks, dtype=jnp.int32)
    distance = reach - jnp.arange(CYCLE, dtype=jnp.int32)
    used = jnp.arange(CYCLE, dtype=jnp.int32)[None, :] < block_counts[:, None]
    hits = used[:, None, :] & (block_lists[:, None, :] == (target[:, None] - distance[None, :])[:, :, None])
    flags = jnp.any(hits, axis=2).astype(jnp.int32)
    joined = pl.pallas_call(
        attention_kernel,
        out_shape=jax.ShapeDtypeStruct((rows, mine.shape[2]), queries.dtype),
        in_specs=[
            pl.BlockSpec(memory_space=pltpu.SMEM),
            pl.BlockSpec(memory_space=pltpu.VMEM),
            pl.BlockSpec(memory_space=pltpu.VMEM),
        ],
        out_specs=pl.BlockSpec(memory_space=pltpu.VMEM),
    )(flags, mine, before)
    return lax.all_to_all(joined, "head", split_axis=0, concat_axis=1, tiled=True)


def solution(mesh):
    return jax.shard_map(
        body,
        mesh=mesh,
        in_specs=(
            P(("blk", "head"), None),
            P(("blk", "head"), None),
            P(("blk", "head"), None),
            P("blk", None),
            P("blk"),
        ),
        out_specs=P(("blk", "head"), None),
        check_vma=False,
    )
```

```python
import jax
import jax.numpy as jnp
from jax import lax
from jax.experimental import pallas as pl
from jax.experimental.pallas import tpu as pltpu
from jax.sharding import PartitionSpec as P

HEADS = 32
HDIM = 128
BLOCK = 256
CYCLE = 3


def from_behind(value, axis, steps):
    count = lax.axis_size(axis)
    initial, last = (max(0, -steps), min(count, count - steps))
    return lax.ppermute(value, axis, [(source, source + steps) for source in range(initial, last)])


def attention_kernel(flags_ref, q_ref, kv_ref, before_ref, out_ref):
    peers, chunk, width = q_ref.shape
    per_block = BLOCK // chunk
    owned_blocks = peers // per_block
    local_heads = width // HDIM
    reach = CYCLE - 1
    scale = 1.0 / HDIM**0.5
    row_pos = lax.broadcasted_iota(jnp.int32, (BLOCK, BLOCK), 0)
    col_pos = lax.broadcasted_iota(jnp.int32, (BLOCK, BLOCK), 1)
    causal = col_pos <= row_pos
    for local in range(owned_blocks):
        wanted = [flags_ref[local, place] != 0 for place in range(CYCLE)]
        masks = []
        for place in range(CYCLE):
            if place == reach:
                masks.append(causal & wanted[place])
            else:
                masks.append(jnp.broadcast_to(wanted[place], (BLOCK, BLOCK)))
        rows = slice(local * per_block, (local + 1) * per_block)
        for head in range(local_heads):
            cols = slice(head * HDIM, (head + 1) * HDIM)
            q = q_ref[rows, :, cols].reshape(BLOCK, HDIM)
            parts = []
            for place in range(CYCLE):
                source = local - (reach - place)
                if source >= 0:
                    src = slice(source * per_block, (source + 1) * per_block)
                    k = kv_ref[src, 0, :, cols].reshape(BLOCK, HDIM)
                    v = kv_ref[src, 1, :, cols].reshape(BLOCK, HDIM)
                else:
                    src = slice((source + reach) * per_block, (source + reach + 1) * per_block)
                    k = before_ref[src, 0, :, cols].reshape(BLOCK, HDIM)
                    v = before_ref[src, 1, :, cols].reshape(BLOCK, HDIM)
                s = lax.dot_general(q, k, (((1,), (1,)), ((), ())), preferred_element_type=jnp.float32) * scale
                s = jnp.where(masks[place], s, -1e30)
                parts.append((s, v))
            top = jnp.max(parts[0][0], axis=1, keepdims=True)
            for s, _ in parts[1:]:
                top = jnp.maximum(top, jnp.max(s, axis=1, keepdims=True))
            total = None
            summed = None
            for place, (s, v) in enumerate(parts):
                w = jnp.where(masks[place], jnp.exp(s - top), 0.0)
                t = jnp.sum(w, axis=1, keepdims=True)
                o = jnp.dot(w.astype(jnp.bfloat16), v, preferred_element_type=jnp.float32)
                total = t if total is None else total + t
                summed = o if summed is None else summed + o
            result = (summed / total).astype(out_ref.dtype)
            out_ref[rows, :, cols] = result.reshape(per_block, chunk, HDIM)


def body(queries, keys, values, block_lists, block_counts):
    peers = lax.axis_size("head")
    chunk, width = queries.shape
    cols = width // peers
    per_block = BLOCK // chunk
    owned_blocks = peers // per_block
    reach = CYCLE - 1
    kv_out = jnp.stack((keys, values)).reshape(2, chunk, peers, cols).transpose(2, 0, 1, 3)
    kv = lax.all_to_all(kv_out, "head", split_axis=0, concat_axis=0, tiled=True)
    before = from_behind(kv[peers - reach * per_block :], "blk", 1)
    q_out = queries.reshape(chunk, peers, cols).transpose(1, 0, 2)
    q = lax.all_to_all(q_out, "head", split_axis=0, concat_axis=0, tiled=True)
    own = lax.axis_index("blk")
    target = own * owned_blocks + jnp.arange(owned_blocks, dtype=jnp.int32)
    distance = reach - jnp.arange(CYCLE, dtype=jnp.int32)
    used = jnp.arange(CYCLE, dtype=jnp.int32)[None, :] < block_counts[:, None]
    hits = used[:, None, :] & (block_lists[:, None, :] == (target[:, None] - distance[None, :])[:, :, None])
    flags = jnp.any(hits, axis=2).astype(jnp.int32)
    joined = pl.pallas_call(
        attention_kernel,
        out_shape=jax.ShapeDtypeStruct(q.shape, queries.dtype),
        in_specs=[
            pl.BlockSpec(memory_space=pltpu.SMEM),
            pl.BlockSpec(memory_space=pltpu.VMEM),
            pl.BlockSpec(memory_space=pltpu.VMEM),
            pl.BlockSpec(memory_space=pltpu.VMEM),
        ],
        out_specs=pl.BlockSpec(memory_space=pltpu.VMEM),
    )(flags, q, kv, before)
    back = lax.all_to_all(joined, "head", split_axis=0, concat_axis=0, tiled=True)
    return back.transpose(1, 0, 2).reshape(chunk, width)


def solution(mesh):
    return jax.shard_map(
        body,
        mesh=mesh,
        in_specs=(
            P(("blk", "head"), None),
            P(("blk", "head"), None),
            P(("blk", "head"), None),
            P("blk", None),
            P("blk"),
        ),
        out_specs=P(("blk", "head"), None),
        check_vma=False,
    )
```

```python
import functools

import jax
import jax.numpy as jnp
from jax import lax
from jax.experimental import pallas as pl
from jax.experimental.pallas import tpu as pltpu
from jax.sharding import PartitionSpec as P

HEADS = 32
HDIM = 128
BLOCK = 256
CYCLE = 3


def from_behind(value, axis, steps):
    count = lax.axis_size(axis)
    initial, last = (max(0, -steps), min(count, count - steps))
    return lax.ppermute(value, axis, [(source, source + steps) for source in range(initial, last)])


def attention_kernel(blocks, has_before, has_prior, flags_ref, qkv_ref, *refs):
    before_ref = refs[0] if has_before else None
    out_ref = refs[-1]
    peers, _, chunk, width = qkv_ref.shape
    per_block = BLOCK // chunk
    local_heads = width // HDIM
    reach = CYCLE - 1
    scale = 1.0 / HDIM**0.5
    row_pos = lax.broadcasted_iota(jnp.int32, (BLOCK, BLOCK), 0)
    col_pos = lax.broadcasted_iota(jnp.int32, (BLOCK, BLOCK), 1)
    causal = col_pos <= row_pos
    if has_prior:
        prior_ref = refs[-2]
        for local in range(peers // per_block):
            if local not in blocks:
                rows = slice(local * per_block, (local + 1) * per_block)
                out_ref[rows] = prior_ref[rows]
    for local in blocks:
        wanted = [flags_ref[local, place] != 0 for place in range(CYCLE)]
        masks = []
        for place in range(CYCLE):
            if place == reach:
                masks.append(causal & wanted[place])
            else:
                masks.append(jnp.broadcast_to(wanted[place], (BLOCK, BLOCK)))
        rows = slice(local * per_block, (local + 1) * per_block)
        for head in range(local_heads):
            cols = slice(head * HDIM, (head + 1) * HDIM)
            q = qkv_ref[rows, 0, :, cols].reshape(BLOCK, HDIM)
            parts = []
            for place in range(CYCLE):
                source = local - (reach - place)
                if source >= 0:
                    src = slice(source * per_block, (source + 1) * per_block)
                    k = qkv_ref[src, 1, :, cols].reshape(BLOCK, HDIM)
                    v = qkv_ref[src, 2, :, cols].reshape(BLOCK, HDIM)
                else:
                    src = slice((source + reach) * per_block, (source + reach + 1) * per_block)
                    k = before_ref[src, 0, :, cols].reshape(BLOCK, HDIM)
                    v = before_ref[src, 1, :, cols].reshape(BLOCK, HDIM)
                s = lax.dot_general(q, k, (((1,), (1,)), ((), ())), preferred_element_type=jnp.float32) * scale
                s = jnp.where(masks[place], s, -1e30)
                parts.append((s, v))
            top = jnp.max(parts[0][0], axis=1, keepdims=True)
            for s, _ in parts[1:]:
                top = jnp.maximum(top, jnp.max(s, axis=1, keepdims=True))
            total = None
            summed = None
            for place, (s, v) in enumerate(parts):
                w = jnp.where(masks[place], jnp.exp(s - top), 0.0)
                t = jnp.sum(w, axis=1, keepdims=True)
                o = jnp.dot(w.astype(jnp.bfloat16), v, preferred_element_type=jnp.float32)
                total = t if total is None else total + t
                summed = o if summed is None else summed + o
            result = (summed / total).astype(out_ref.dtype)
            out_ref[rows, :, cols] = result.reshape(per_block, chunk, HDIM)


def attend(blocks, flags, qkv, before, prior):
    vmem = pl.BlockSpec(memory_space=pltpu.VMEM)
    extra = tuple(x for x in (before, prior) if x is not None)
    peers, _, chunk, width = qkv.shape
    return pl.pallas_call(
        functools.partial(attention_kernel, blocks, before is not None, prior is not None),
        out_shape=jax.ShapeDtypeStruct((peers, chunk, width), qkv.dtype),
        in_specs=[pl.BlockSpec(memory_space=pltpu.SMEM)] + [vmem] * (1 + len(extra)),
        out_specs=vmem,
    )(flags, qkv, *extra)


def body(queries, keys, values, block_lists, block_counts):
    peers = lax.axis_size("head")
    chunk, width = queries.shape
    cols = width // peers
    per_block = BLOCK // chunk
    owned_blocks = peers // per_block
    reach = CYCLE - 1
    qkv_out = jnp.stack((queries, keys, values)).reshape(3, chunk, peers, cols).transpose(2, 0, 1, 3)
    qkv = lax.all_to_all(qkv_out, "head", split_axis=0, concat_axis=0, tiled=True)
    before = from_behind(qkv[peers - reach * per_block :, 1:], "blk", 1)
    own = lax.axis_index("blk")
    target = own * owned_blocks + jnp.arange(owned_blocks, dtype=jnp.int32)
    distance = reach - jnp.arange(CYCLE, dtype=jnp.int32)
    used = jnp.arange(CYCLE, dtype=jnp.int32)[None, :] < block_counts[:, None]
    hits = used[:, None, :] & (block_lists[:, None, :] == (target[:, None] - distance[None, :])[:, :, None])
    flags = jnp.any(hits, axis=2).astype(jnp.int32)
    late = tuple(range(min(reach, owned_blocks)))
    early = tuple(range(len(late), owned_blocks))
    joined = attend(early, flags, qkv, None, None) if early else None
    joined = attend(late, flags, qkv, before, joined)
    back = lax.all_to_all(joined, "head", split_axis=0, concat_axis=0, tiled=True)
    return back.transpose(1, 0, 2).reshape(chunk, width)


def solution(mesh):
    return jax.shard_map(
        body,
        mesh=mesh,
        in_specs=(
            P(("blk", "head"), None),
            P(("blk", "head"), None),
            P(("blk", "head"), None),
            P("blk", None),
            P("blk"),
        ),
        out_specs=P(("blk", "head"), None),
        check_vma=False,
    )
```

```python
import functools

import jax
import jax.numpy as jnp
from jax import lax
from jax.experimental import pallas as pl
from jax.experimental.pallas import tpu as pltpu
from jax.sharding import PartitionSpec as P

HEADS = 32
HDIM = 128
BLOCK = 256
CYCLE = 3


def from_behind(value, axis, steps):
    count = lax.axis_size(axis)
    initial, last = (max(0, -steps), min(count, count - steps))
    return lax.ppermute(value, axis, [(source, source + steps) for source in range(initial, last)])


def attention_kernel(blocks, has_before, has_prior, flags_ref, qkv_ref, *refs):
    before_ref = refs[0] if has_before else None
    out_ref = refs[-1]
    peers, _, chunk, width = qkv_ref.shape
    per_block = BLOCK // chunk
    local_heads = width // HDIM
    reach = CYCLE - 1
    scale = 1.0 / HDIM**0.5
    row_pos = lax.broadcasted_iota(jnp.int32, (BLOCK, BLOCK), 0)
    col_pos = lax.broadcasted_iota(jnp.int32, (BLOCK, BLOCK), 1)
    causal = col_pos <= row_pos
    if has_prior:
        prior_ref = refs[-2]
        for local in range(peers // per_block):
            if local not in blocks:
                rows = slice(local * per_block, (local + 1) * per_block)
                out_ref[rows] = prior_ref[rows]
    for local in blocks:
        wanted = [flags_ref[local, place] != 0 for place in range(CYCLE)]
        masks = []
        for place in range(CYCLE):
            if place == reach:
                masks.append(causal & wanted[place])
            else:
                masks.append(jnp.broadcast_to(wanted[place], (BLOCK, BLOCK)))
        rows = slice(local * per_block, (local + 1) * per_block)
        for head in range(local_heads):
            cols = slice(head * HDIM, (head + 1) * HDIM)
            q = qkv_ref[rows, 0, :, cols].reshape(BLOCK, HDIM)
            parts = []
            for place in range(CYCLE):
                source = local - (reach - place)
                if source >= 0:
                    src = slice(source * per_block, (source + 1) * per_block)
                    k = qkv_ref[src, 1, :, cols].reshape(BLOCK, HDIM)
                    v = qkv_ref[src, 2, :, cols].reshape(BLOCK, HDIM)
                else:
                    src = slice((source + reach) * per_block, (source + reach + 1) * per_block)
                    k = before_ref[src, 0, :, cols].reshape(BLOCK, HDIM)
                    v = before_ref[src, 1, :, cols].reshape(BLOCK, HDIM)
                s = lax.dot_general(q, k, (((1,), (1,)), ((), ())), preferred_element_type=jnp.float32) * scale
                s = jnp.where(masks[place], s, -1e30)
                parts.append((s, v))
            top = jnp.max(parts[0][0], axis=1, keepdims=True)
            for s, _ in parts[1:]:
                top = jnp.maximum(top, jnp.max(s, axis=1, keepdims=True))
            total = None
            summed = None
            for place, (s, v) in enumerate(parts):
                w = jnp.where(masks[place], jnp.exp(s - top), 0.0)
                t = jnp.sum(w, axis=1, keepdims=True)
                o = jnp.dot(w.astype(jnp.bfloat16), v, preferred_element_type=jnp.float32)
                total = t if total is None else total + t
                summed = o if summed is None else summed + o
            result = (summed / total).astype(out_ref.dtype)
            out_ref[rows, :, cols] = result.reshape(per_block, chunk, HDIM)


def attend(blocks, flags, qkv, before, prior):
    vmem = pl.BlockSpec(memory_space=pltpu.VMEM)
    extra = tuple(x for x in (before, prior) if x is not None)
    peers, _, chunk, width = qkv.shape
    return pl.pallas_call(
        functools.partial(attention_kernel, blocks, before is not None, prior is not None),
        out_shape=jax.ShapeDtypeStruct((peers, chunk, width), qkv.dtype),
        in_specs=[pl.BlockSpec(memory_space=pltpu.SMEM)] + [vmem] * (1 + len(extra)),
        out_specs=vmem,
    )(flags, qkv, *extra)


def body(queries, keys, values, block_lists, block_counts):
    peers = lax.axis_size("head")
    chunk, width = queries.shape
    cols = width // peers
    local_heads = cols // HDIM
    per_block = BLOCK // chunk
    owned_blocks = peers // per_block
    reach = CYCLE - 1
    own = lax.axis_index("blk")
    target = own * owned_blocks + jnp.arange(owned_blocks, dtype=jnp.int32)
    distance = reach - jnp.arange(CYCLE, dtype=jnp.int32)
    used = jnp.arange(CYCLE, dtype=jnp.int32)[None, :] < block_counts[:, None]
    hits = used[:, None, :] & (block_lists[:, None, :] == (target[:, None] - distance[None, :])[:, :, None])
    flags = jnp.any(hits, axis=2).astype(jnp.int32)
    stacked = jnp.stack((queries, keys, values)).reshape(3, chunk, peers, local_heads, HDIM)
    outgoing = stacked.transpose(3, 2, 0, 1, 4)
    results = []
    for head in range(local_heads):
        qkv = lax.all_to_all(outgoing[head], "head", split_axis=0, concat_axis=0, tiled=True)
        before = from_behind(qkv[peers - reach * per_block :, 1:], "blk", 1)
        joined = attend(tuple(range(owned_blocks)), flags, qkv, before, None)
        results.append(lax.all_to_all(joined, "head", split_axis=0, concat_axis=0, tiled=True))
    back = jnp.stack(results, axis=2)
    return back.transpose(1, 0, 2, 3).reshape(chunk, width)


def solution(mesh):
    return jax.shard_map(
        body,
        mesh=mesh,
        in_specs=(
            P(("blk", "head"), None),
            P(("blk", "head"), None),
            P(("blk", "head"), None),
            P("blk", None),
            P("blk"),
        ),
        out_specs=P(("blk", "head"), None),
        check_vma=False,
    )
```

```python
import jax
import jax.numpy as jnp
from jax import lax
from jax.experimental import pallas as pl
from jax.experimental.pallas import tpu as pltpu
from jax.sharding import PartitionSpec as P

HEADS = 32
HDIM = 128
BLOCK = 256
CYCLE = 3


def from_behind(value, axis, steps):
    count = lax.axis_size(axis)
    initial, last = (max(0, -steps), min(count, count - steps))
    return lax.ppermute(value, axis, [(source, source + steps) for source in range(initial, last)])


def attention_kernel(flags_ref, slots_ref, qkv_ref, before_ref, out_ref):
    peers, _, chunk, width = qkv_ref.shape
    per_block = BLOCK // chunk
    owned_blocks = peers // per_block
    local_heads = width // HDIM
    reach = CYCLE - 1
    halo = reach * per_block
    scale = 1.0 / HDIM**0.5
    row_pos = lax.broadcasted_iota(jnp.int32, (BLOCK, BLOCK), 0)
    col_pos = lax.broadcasted_iota(jnp.int32, (BLOCK, BLOCK), 1)
    causal = col_pos <= row_pos

    def gather(ref, first, t, cols, wrap):
        pieces = []
        for part in range(per_block):
            slot = slots_ref[first + part]
            if wrap:
                slot = slot % halo
            pieces.append(ref[slot, t, :, cols])
        return jnp.concatenate(pieces, axis=0)

    for local in range(owned_blocks):
        wanted = [flags_ref[local, place] != 0 for place in range(CYCLE)]
        masks = []
        for place in range(CYCLE):
            if place == reach:
                masks.append(causal & wanted[place])
            else:
                masks.append(jnp.broadcast_to(wanted[place], (BLOCK, BLOCK)))
        for head in range(local_heads):
            cols = slice(head * HDIM, (head + 1) * HDIM)
            q = gather(qkv_ref, local * per_block, 0, cols, False)
            parts = []
            for place in range(CYCLE):
                source = local - (reach - place)
                if source >= 0:
                    k = gather(qkv_ref, source * per_block, 1, cols, False)
                    v = gather(qkv_ref, source * per_block, 2, cols, False)
                else:
                    first = (source + owned_blocks) * per_block
                    k = gather(before_ref, first, 0, cols, True)
                    v = gather(before_ref, first, 1, cols, True)
                s = lax.dot_general(q, k, (((1,), (1,)), ((), ())), preferred_element_type=jnp.float32) * scale
                s = jnp.where(masks[place], s, -1e30)
                parts.append((s, v))
            top = jnp.max(parts[0][0], axis=1, keepdims=True)
            for s, _ in parts[1:]:
                top = jnp.maximum(top, jnp.max(s, axis=1, keepdims=True))
            total = None
            summed = None
            for place, (s, v) in enumerate(parts):
                w = jnp.where(masks[place], jnp.exp(s - top), 0.0)
                t = jnp.sum(w, axis=1, keepdims=True)
                o = jnp.dot(w.astype(jnp.bfloat16), v, preferred_element_type=jnp.float32)
                total = t if total is None else total + t
                summed = o if summed is None else summed + o
            result = (summed / total).astype(out_ref.dtype)
            for part in range(per_block):
                slot = slots_ref[local * per_block + part]
                out_ref[slot, :, cols] = result[part * chunk : (part + 1) * chunk]


def exchange(slabs, me, axis):
    peers = slabs.shape[0]
    got = [lax.dynamic_index_in_dim(slabs, me, 0, keepdims=False)]
    for step in range(1, peers):
        send = lax.dynamic_index_in_dim(slabs, me ^ step, 0, keepdims=False)
        got.append(lax.ppermute(send, axis, [(j, j ^ step) for j in range(peers)]))
    return jnp.stack(got)


def body(queries, keys, values, block_lists, block_counts):
    peers = lax.axis_size("head")
    chunk, width = queries.shape
    cols = width // peers
    per_block = BLOCK // chunk
    owned_blocks = peers // per_block
    reach = CYCLE - 1
    halo = reach * per_block
    own = lax.axis_index("blk")
    me = lax.axis_index("head").astype(jnp.int32)
    target = own * owned_blocks + jnp.arange(owned_blocks, dtype=jnp.int32)
    distance = reach - jnp.arange(CYCLE, dtype=jnp.int32)
    used = jnp.arange(CYCLE, dtype=jnp.int32)[None, :] < block_counts[:, None]
    hits = used[:, None, :] & (block_lists[:, None, :] == (target[:, None] - distance[None, :])[:, :, None])
    flags = jnp.any(hits, axis=2).astype(jnp.int32)
    slots = jnp.bitwise_xor(me, jnp.arange(peers, dtype=jnp.int32))
    outgoing = jnp.stack((queries, keys, values)).reshape(3, chunk, peers, cols).transpose(2, 0, 1, 3)
    qkv = exchange(outgoing, me, "head")
    tail = lax.dynamic_slice_in_dim(qkv[:, 1:], slots[peers - halo] - slots[peers - halo] % halo, halo, 0)
    before = from_behind(tail, "blk", 1)
    vmem = pl.BlockSpec(memory_space=pltpu.VMEM)
    smem = pl.BlockSpec(memory_space=pltpu.SMEM)
    joined = pl.pallas_call(
        attention_kernel,
        out_shape=jax.ShapeDtypeStruct((peers, chunk, cols), queries.dtype),
        in_specs=[smem, smem, vmem, vmem],
        out_specs=vmem,
    )(flags, slots, qkv, before)
    back = exchange(joined, jnp.int32(0), "head")
    ordered = jnp.take(back, slots, axis=0)
    return ordered.transpose(1, 0, 2).reshape(chunk, width)


def solution(mesh):
    return jax.shard_map(
        body,
        mesh=mesh,
        in_specs=(
            P(("blk", "head"), None),
            P(("blk", "head"), None),
            P(("blk", "head"), None),
            P("blk", None),
            P("blk"),
        ),
        out_specs=P(("blk", "head"), None),
        check_vma=False,
    )
```

```python
import functools

import jax
import jax.numpy as jnp
from jax import lax
from jax.experimental import pallas as pl
from jax.experimental.pallas import tpu as pltpu
from jax.sharding import PartitionSpec as P

HEADS = 32
HDIM = 128
BLOCK = 256
CYCLE = 3


def from_behind(value, axis, steps):
    count = lax.axis_size(axis)
    initial, last = (max(0, -steps), min(count, count - steps))
    return lax.ppermute(value, axis, [(source, source + steps) for source in range(initial, last)])


def attention_kernel(blocks, has_before, has_prior, flags_ref, qkv_ref, *refs):
    before_ref = refs[0] if has_before else None
    out_ref = refs[-1]
    peers, _, chunk, width = qkv_ref.shape
    per_block = BLOCK // chunk
    local_heads = width // HDIM
    reach = CYCLE - 1
    scale = 1.0 / HDIM**0.5
    row_pos = lax.broadcasted_iota(jnp.int32, (BLOCK, BLOCK), 0)
    col_pos = lax.broadcasted_iota(jnp.int32, (BLOCK, BLOCK), 1)
    causal = col_pos <= row_pos
    if has_prior:
        prior_ref = refs[-2]
        for local in range(peers // per_block):
            if local not in blocks:
                rows = slice(local * per_block, (local + 1) * per_block)
                out_ref[rows] = prior_ref[rows]
    for local in blocks:
        wanted = [flags_ref[local, place] != 0 for place in range(CYCLE)]
        masks = []
        for place in range(CYCLE):
            if place == reach:
                masks.append(causal & wanted[place])
            else:
                masks.append(jnp.broadcast_to(wanted[place], (BLOCK, BLOCK)))
        rows = slice(local * per_block, (local + 1) * per_block)
        for head in range(local_heads):
            cols = slice(head * HDIM, (head + 1) * HDIM)
            q = qkv_ref[rows, 0, :, cols].reshape(BLOCK, HDIM)
            parts = []
            for place in range(CYCLE):
                source = local - (reach - place)
                if source >= 0:
                    src = slice(source * per_block, (source + 1) * per_block)
                    k = qkv_ref[src, 1, :, cols].reshape(BLOCK, HDIM)
                    v = qkv_ref[src, 2, :, cols].reshape(BLOCK, HDIM)
                else:
                    src = slice((source + reach) * per_block, (source + reach + 1) * per_block)
                    k = before_ref[src, 0, :, cols].reshape(BLOCK, HDIM)
                    v = before_ref[src, 1, :, cols].reshape(BLOCK, HDIM)
                s = lax.dot_general(q, k, (((1,), (1,)), ((), ())), preferred_element_type=jnp.float32) * scale
                s = jnp.where(masks[place], s, -1e30)
                parts.append((s, v))
            top = jnp.max(parts[0][0], axis=1, keepdims=True)
            for s, _ in parts[1:]:
                top = jnp.maximum(top, jnp.max(s, axis=1, keepdims=True))
            total = None
            summed = None
            for place, (s, v) in enumerate(parts):
                w = jnp.exp(s - top)
                t = jnp.sum(w, axis=1, keepdims=True)
                o = jnp.dot(w.astype(jnp.bfloat16), v, preferred_element_type=jnp.float32)
                total = t if total is None else total + t
                summed = o if summed is None else summed + o
            result = (summed / total).astype(out_ref.dtype)
            out_ref[rows, :, cols] = result.reshape(per_block, chunk, HDIM)


def slab_kernel(q_ref, k_ref, v_ref, out_ref):
    peers, _, _, cols = out_ref.shape
    for t, ref in enumerate((q_ref, k_ref, v_ref)):
        for dest in range(peers):
            out_ref[dest, t] = ref[:, dest * cols : (dest + 1) * cols]


def attend(blocks, flags, qkv, before, prior):
    vmem = pl.BlockSpec(memory_space=pltpu.VMEM)
    extra = tuple(x for x in (before, prior) if x is not None)
    peers, _, chunk, width = qkv.shape
    return pl.pallas_call(
        functools.partial(attention_kernel, blocks, before is not None, prior is not None),
        out_shape=jax.ShapeDtypeStruct((peers, chunk, width), qkv.dtype),
        in_specs=[pl.BlockSpec(memory_space=pltpu.SMEM)] + [vmem] * (1 + len(extra)),
        out_specs=vmem,
    )(flags, qkv, *extra)


def body(queries, keys, values, block_lists, block_counts):
    peers = lax.axis_size("head")
    chunk, width = queries.shape
    cols = width // peers
    per_block = BLOCK // chunk
    owned_blocks = peers // per_block
    reach = CYCLE - 1
    qkv_out = pl.pallas_call(
        slab_kernel,
        out_shape=jax.ShapeDtypeStruct((peers, 3, chunk, cols), queries.dtype),
        in_specs=[pl.BlockSpec(memory_space=pltpu.VMEM)] * 3,
        out_specs=pl.BlockSpec(memory_space=pltpu.VMEM),
    )(queries, keys, values)
    qkv = lax.all_to_all(qkv_out, "head", split_axis=0, concat_axis=0, tiled=True)
    before = from_behind(qkv[peers - reach * per_block :, 1:], "blk", 1)
    own = lax.axis_index("blk")
    target = own * owned_blocks + jnp.arange(owned_blocks, dtype=jnp.int32)
    distance = reach - jnp.arange(CYCLE, dtype=jnp.int32)
    used = jnp.arange(CYCLE, dtype=jnp.int32)[None, :] < block_counts[:, None]
    hits = used[:, None, :] & (block_lists[:, None, :] == (target[:, None] - distance[None, :])[:, :, None])
    flags = jnp.any(hits, axis=2).astype(jnp.int32)
    late = tuple(range(min(reach, owned_blocks)))
    early = tuple(range(len(late), owned_blocks))
    joined = attend(early, flags, qkv, None, None) if early else None
    joined = attend(late, flags, qkv, before, joined)
    back = lax.all_to_all(joined, "head", split_axis=0, concat_axis=0, tiled=True)
    return back.transpose(1, 0, 2).reshape(chunk, width)


def solution(mesh):
    return jax.shard_map(
        body,
        mesh=mesh,
        in_specs=(
            P(("blk", "head"), None),
            P(("blk", "head"), None),
            P(("blk", "head"), None),
            P("blk", None),
            P("blk"),
        ),
        out_specs=P(("blk", "head"), None),
        check_vma=False,
    )
```

```python
import functools

import jax
import jax.numpy as jnp
from jax import lax
from jax.experimental import pallas as pl
from jax.experimental.pallas import tpu as pltpu
from jax.sharding import PartitionSpec as P

HEADS = 32
HDIM = 128
BLOCK = 256
CYCLE = 3


def from_behind(value, axis, steps):
    count = lax.axis_size(axis)
    initial, last = (max(0, -steps), min(count, count - steps))
    return lax.ppermute(value, axis, [(source, source + steps) for source in range(initial, last)])


def attention_kernel(blocks, has_before, flags_ref, qkv_ref, *refs):
    before_ref = refs[0] if has_before else None
    out_ref = refs[-1]
    _, _, chunk, width = qkv_ref.shape
    per_block = BLOCK // chunk
    out_first = blocks[0] * per_block
    local_heads = width // HDIM
    reach = CYCLE - 1
    scale = 1.0 / HDIM**0.5
    row_pos = lax.broadcasted_iota(jnp.int32, (BLOCK, BLOCK), 0)
    col_pos = lax.broadcasted_iota(jnp.int32, (BLOCK, BLOCK), 1)
    causal = col_pos <= row_pos
    for local in blocks:
        wanted = [flags_ref[local, place] != 0 for place in range(CYCLE)]
        masks = []
        for place in range(CYCLE):
            if place == reach:
                masks.append(causal & wanted[place])
            else:
                masks.append(jnp.broadcast_to(wanted[place], (BLOCK, BLOCK)))
        rows = slice(local * per_block, (local + 1) * per_block)
        for head in range(local_heads):
            cols = slice(head * HDIM, (head + 1) * HDIM)
            q = qkv_ref[rows, 0, :, cols].reshape(BLOCK, HDIM)
            parts = []
            for place in range(CYCLE):
                source = local - (reach - place)
                if source >= 0:
                    src = slice(source * per_block, (source + 1) * per_block)
                    k = qkv_ref[src, 1, :, cols].reshape(BLOCK, HDIM)
                    v = qkv_ref[src, 2, :, cols].reshape(BLOCK, HDIM)
                else:
                    src = slice((source + reach) * per_block, (source + reach + 1) * per_block)
                    k = before_ref[src, 0, :, cols].reshape(BLOCK, HDIM)
                    v = before_ref[src, 1, :, cols].reshape(BLOCK, HDIM)
                s = lax.dot_general(q, k, (((1,), (1,)), ((), ())), preferred_element_type=jnp.float32) * scale
                s = jnp.where(masks[place], s, -1e30)
                parts.append((s, v))
            top = jnp.max(parts[0][0], axis=1, keepdims=True)
            for s, _ in parts[1:]:
                top = jnp.maximum(top, jnp.max(s, axis=1, keepdims=True))
            total = None
            summed = None
            for place, (s, v) in enumerate(parts):
                w = jnp.exp(s - top)
                t = jnp.sum(w, axis=1, keepdims=True)
                o = jnp.dot(w.astype(jnp.bfloat16), v, preferred_element_type=jnp.float32)
                total = t if total is None else total + t
                summed = o if summed is None else summed + o
            result = (summed / total).astype(out_ref.dtype)
            out_rows = slice(local * per_block - out_first, (local + 1) * per_block - out_first)
            out_ref[out_rows, :, cols] = result.reshape(per_block, chunk, HDIM)


def slab_kernel(q_ref, k_ref, v_ref, out_ref):
    peers, _, _, cols = out_ref.shape
    for t, ref in enumerate((q_ref, k_ref, v_ref)):
        for dest in range(peers):
            out_ref[dest, t] = ref[:, dest * cols : (dest + 1) * cols]


def attend(blocks, flags, qkv, before, prior):
    peers, _, chunk, width = qkv.shape
    per_block = BLOCK // chunk
    rows = len(blocks) * per_block
    reads = (blocks[-1] + 1) * per_block if blocks[0] == 0 else peers
    operands = [flags, qkv]
    in_specs = [
        pl.BlockSpec(memory_space=pltpu.SMEM),
        pl.BlockSpec((reads,) + qkv.shape[1:], lambda i: (0, 0, 0, 0)),
    ]
    if before is not None:
        operands.append(before)
        in_specs.append(pl.BlockSpec(before.shape, lambda i: (0, 0, 0, 0)))
    aliases = {}
    if prior is not None:
        aliases = {len(operands): 0}
        operands.append(prior)
        in_specs.append(pl.BlockSpec(memory_space=pl.ANY))
    return pl.pallas_call(
        functools.partial(attention_kernel, blocks, before is not None),
        out_shape=jax.ShapeDtypeStruct((peers, chunk, width), qkv.dtype),
        grid=(1,),
        in_specs=in_specs,
        out_specs=pl.BlockSpec((rows, chunk, width), lambda i: (blocks[0] * per_block // rows, 0, 0)),
        input_output_aliases=aliases,
    )(*operands)


def body(queries, keys, values, block_lists, block_counts):
    peers = lax.axis_size("head")
    chunk, width = queries.shape
    cols = width // peers
    per_block = BLOCK // chunk
    owned_blocks = peers // per_block
    reach = CYCLE - 1
    qkv_out = pl.pallas_call(
        slab_kernel,
        out_shape=jax.ShapeDtypeStruct((peers, 3, chunk, cols), queries.dtype),
        in_specs=[pl.BlockSpec(memory_space=pltpu.VMEM)] * 3,
        out_specs=pl.BlockSpec(memory_space=pltpu.VMEM),
    )(queries, keys, values)
    qkv = lax.all_to_all(qkv_out, "head", split_axis=0, concat_axis=0, tiled=True)
    before = from_behind(qkv[peers - reach * per_block :, 1:], "blk", 1)
    own = lax.axis_index("blk")
    target = own * owned_blocks + jnp.arange(owned_blocks, dtype=jnp.int32)
    distance = reach - jnp.arange(CYCLE, dtype=jnp.int32)
    used = jnp.arange(CYCLE, dtype=jnp.int32)[None, :] < block_counts[:, None]
    hits = used[:, None, :] & (block_lists[:, None, :] == (target[:, None] - distance[None, :])[:, :, None])
    flags = jnp.any(hits, axis=2).astype(jnp.int32)
    late = tuple(range(min(reach, owned_blocks)))
    early = tuple(range(len(late), owned_blocks))
    joined = attend(early, flags, qkv, None, None) if early else None
    joined = attend(late, flags, qkv, before, joined)
    back = lax.all_to_all(joined, "head", split_axis=0, concat_axis=0, tiled=True)
    return back.transpose(1, 0, 2).reshape(chunk, width)


def solution(mesh):
    return jax.shard_map(
        body,
        mesh=mesh,
        in_specs=(
            P(("blk", "head"), None),
            P(("blk", "head"), None),
            P(("blk", "head"), None),
            P("blk", None),
            P("blk"),
        ),
        out_specs=P(("blk", "head"), None),
        check_vma=False,
    )
```

```python
import functools

import jax
import jax.numpy as jnp
from jax import lax
from jax.experimental import pallas as pl
from jax.experimental.pallas import tpu as pltpu
from jax.sharding import PartitionSpec as P

HEADS = 32
HDIM = 128
BLOCK = 256
CYCLE = 3


def from_behind(value, axis, steps):
    count = lax.axis_size(axis)
    initial, last = (max(0, -steps), min(count, count - steps))
    return lax.ppermute(value, axis, [(source, source + steps) for source in range(initial, last)])


def attention_kernel(blocks, has_before, flags_ref, qkv_ref, *refs):
    before_ref = refs[0] if has_before else None
    out_ref = refs[-1]
    _, _, chunk, width = qkv_ref.shape
    per_block = BLOCK // chunk
    out_first = blocks[0] * per_block
    local_heads = width // HDIM
    reach = CYCLE - 1
    scale = 1.0 / HDIM**0.5
    row_pos = lax.broadcasted_iota(jnp.int32, (BLOCK, CYCLE * BLOCK), 0)
    col_pos = lax.broadcasted_iota(jnp.int32, (BLOCK, CYCLE * BLOCK), 1)
    causal = (col_pos < reach * BLOCK) | (col_pos - reach * BLOCK <= row_pos)
    for local in blocks:
        allowed = causal
        for place in range(CYCLE):
            inside = (col_pos >= place * BLOCK) & (col_pos < (place + 1) * BLOCK)
            allowed = allowed & (jnp.logical_not(inside) | (flags_ref[local, place] != 0))
        rows = slice(local * per_block, (local + 1) * per_block)
        first = local - reach
        for head in range(local_heads):
            cols = slice(head * HDIM, (head + 1) * HDIM)
            q = qkv_ref[rows, 0, :, cols].reshape(BLOCK, HDIM)
            if first >= 0:
                span = slice(first * per_block, (local + 1) * per_block)
                k = qkv_ref[span, 1, :, cols].reshape(CYCLE * BLOCK, HDIM)
                v = qkv_ref[span, 2, :, cols].reshape(CYCLE * BLOCK, HDIM)
            else:
                halo = slice((first + reach) * per_block, reach * per_block)
                own = slice(0, (local + 1) * per_block)
                k = jnp.concatenate(
                    (before_ref[halo, 0, :, cols].reshape(-1, HDIM), qkv_ref[own, 1, :, cols].reshape(-1, HDIM)), axis=0
                )
                v = jnp.concatenate(
                    (before_ref[halo, 1, :, cols].reshape(-1, HDIM), qkv_ref[own, 2, :, cols].reshape(-1, HDIM)), axis=0
                )
            s = lax.dot_general(q, k, (((1,), (1,)), ((), ())), preferred_element_type=jnp.float32) * scale
            s = jnp.where(allowed, s, -1e30)
            top = jnp.max(s, axis=1, keepdims=True)
            w = jnp.exp(s - top)
            total = jnp.sum(w, axis=1, keepdims=True)
            summed = jnp.dot(w.astype(jnp.bfloat16), v, preferred_element_type=jnp.float32)
            result = (summed / total).astype(out_ref.dtype)
            out_rows = slice(local * per_block - out_first, (local + 1) * per_block - out_first)
            out_ref[out_rows, :, cols] = result.reshape(per_block, chunk, HDIM)


def slab_kernel(q_ref, k_ref, v_ref, out_ref):
    peers, _, _, cols = out_ref.shape
    for t, ref in enumerate((q_ref, k_ref, v_ref)):
        for dest in range(peers):
            out_ref[dest, t] = ref[:, dest * cols : (dest + 1) * cols]


def attend(blocks, flags, qkv, before, prior):
    peers, _, chunk, width = qkv.shape
    per_block = BLOCK // chunk
    rows = len(blocks) * per_block
    reads = (blocks[-1] + 1) * per_block if blocks[0] == 0 else peers
    operands = [flags, qkv]
    in_specs = [
        pl.BlockSpec(memory_space=pltpu.SMEM),
        pl.BlockSpec((reads,) + qkv.shape[1:], lambda i: (0, 0, 0, 0)),
    ]
    if before is not None:
        operands.append(before)
        in_specs.append(pl.BlockSpec(before.shape, lambda i: (0, 0, 0, 0)))
    aliases = {}
    if prior is not None:
        aliases = {len(operands): 0}
        operands.append(prior)
        in_specs.append(pl.BlockSpec(memory_space=pl.ANY))
    return pl.pallas_call(
        functools.partial(attention_kernel, blocks, before is not None),
        out_shape=jax.ShapeDtypeStruct((peers, chunk, width), qkv.dtype),
        grid=(1,),
        in_specs=in_specs,
        out_specs=pl.BlockSpec((rows, chunk, width), lambda i: (blocks[0] * per_block // rows, 0, 0)),
        input_output_aliases=aliases,
    )(*operands)


def body(queries, keys, values, block_lists, block_counts):
    peers = lax.axis_size("head")
    chunk, width = queries.shape
    cols = width // peers
    per_block = BLOCK // chunk
    owned_blocks = peers // per_block
    reach = CYCLE - 1
    qkv_out = pl.pallas_call(
        slab_kernel,
        out_shape=jax.ShapeDtypeStruct((peers, 3, chunk, cols), queries.dtype),
        in_specs=[pl.BlockSpec(memory_space=pltpu.VMEM)] * 3,
        out_specs=pl.BlockSpec(memory_space=pltpu.VMEM),
    )(queries, keys, values)
    qkv = lax.all_to_all(qkv_out, "head", split_axis=0, concat_axis=0, tiled=True)
    before = from_behind(qkv[peers - reach * per_block :, 1:], "blk", 1)
    own = lax.axis_index("blk")
    target = own * owned_blocks + jnp.arange(owned_blocks, dtype=jnp.int32)
    distance = reach - jnp.arange(CYCLE, dtype=jnp.int32)
    used = jnp.arange(CYCLE, dtype=jnp.int32)[None, :] < block_counts[:, None]
    hits = used[:, None, :] & (block_lists[:, None, :] == (target[:, None] - distance[None, :])[:, :, None])
    flags = jnp.any(hits, axis=2).astype(jnp.int32)
    late = tuple(range(min(reach, owned_blocks)))
    early = tuple(range(len(late), owned_blocks))
    joined = attend(early, flags, qkv, None, None) if early else None
    joined = attend(late, flags, qkv, before, joined)
    back = lax.all_to_all(joined, "head", split_axis=0, concat_axis=0, tiled=True)
    return back.transpose(1, 0, 2).reshape(chunk, width)


def solution(mesh):
    return jax.shard_map(
        body,
        mesh=mesh,
        in_specs=(
            P(("blk", "head"), None),
            P(("blk", "head"), None),
            P(("blk", "head"), None),
            P("blk", None),
            P("blk"),
        ),
        out_specs=P(("blk", "head"), None),
        check_vma=False,
    )
```

```python
import functools

import jax
import jax.numpy as jnp
from jax import lax
from jax.experimental import pallas as pl
from jax.experimental.pallas import tpu as pltpu
from jax.sharding import PartitionSpec as P

HEADS = 32
HDIM = 128
BLOCK = 256
CYCLE = 3


def from_behind(value, axis, steps):
    count = lax.axis_size(axis)
    initial, last = (max(0, -steps), min(count, count - steps))
    return lax.ppermute(value, axis, [(source, source + steps) for source in range(initial, last)])


def attention_kernel(blocks, has_before, flags_ref, qkv_ref, *refs):
    before_ref = refs[0] if has_before else None
    out_ref = refs[-1]
    _, _, chunk, width = qkv_ref.shape
    per_block = BLOCK // chunk
    out_first = blocks[0] * per_block
    local_heads = width // HDIM
    reach = CYCLE - 1
    scale = 1.0 / HDIM**0.5
    row_pos = lax.broadcasted_iota(jnp.int32, (BLOCK, CYCLE * BLOCK), 0)
    col_pos = lax.broadcasted_iota(jnp.int32, (BLOCK, CYCLE * BLOCK), 1)
    causal = (col_pos < reach * BLOCK) | (col_pos - reach * BLOCK <= row_pos)
    for local in blocks:
        allowed = causal
        for place in range(CYCLE):
            inside = (col_pos >= place * BLOCK) & (col_pos < (place + 1) * BLOCK)
            allowed = allowed & (jnp.logical_not(inside) | (flags_ref[local, place] != 0))
        rows = slice(local * per_block, (local + 1) * per_block)
        first = local - reach
        for head in range(local_heads):
            cols = slice(head * HDIM, (head + 1) * HDIM)
            q = qkv_ref[rows, 0, :, cols].reshape(BLOCK, HDIM)
            if first >= 0:
                span = slice(first * per_block, (local + 1) * per_block)
                k = qkv_ref[span, 1, :, cols].reshape(CYCLE * BLOCK, HDIM)
                v = qkv_ref[span, 2, :, cols].reshape(CYCLE * BLOCK, HDIM)
            else:
                halo = slice((first + reach) * per_block, reach * per_block)
                own = slice(0, (local + 1) * per_block)
                k = jnp.concatenate(
                    (before_ref[halo, 0, :, cols].reshape(-1, HDIM), qkv_ref[own, 1, :, cols].reshape(-1, HDIM)), axis=0
                )
                v = jnp.concatenate(
                    (before_ref[halo, 1, :, cols].reshape(-1, HDIM), qkv_ref[own, 2, :, cols].reshape(-1, HDIM)), axis=0
                )
            s = lax.dot_general(q, k, (((1,), (1,)), ((), ())), preferred_element_type=jnp.float32) * scale
            s = jnp.where(allowed, s, -1e30)
            top = jnp.max(s, axis=1, keepdims=True)
            w = jnp.exp(s - top)
            total = jnp.sum(w, axis=1, keepdims=True)
            summed = jnp.dot(w.astype(jnp.bfloat16), v, preferred_element_type=jnp.float32)
            result = (summed / total).astype(out_ref.dtype)
            out_rows = slice(local * per_block - out_first, (local + 1) * per_block - out_first)
            out_ref[out_rows, :, cols] = result.reshape(per_block, chunk, HDIM)


def slab_kernel(q_ref, k_ref, v_ref, out_ref):
    group, _, _, cols = out_ref.shape
    for t, ref in enumerate((q_ref, k_ref, v_ref)):
        for dest in range(group):
            out_ref[dest, t] = ref[:, dest * cols : (dest + 1) * cols]


def slabs(queries, keys, values, peers):
    chunk, width = queries.shape
    cols = width // peers
    group = 4 if peers % 4 == 0 else 1
    tensor = pl.BlockSpec((chunk, group * cols), lambda g: (0, g))
    return pl.pallas_call(
        slab_kernel,
        out_shape=jax.ShapeDtypeStruct((peers, 3, chunk, cols), queries.dtype),
        grid=(peers // group,),
        in_specs=[tensor] * 3,
        out_specs=pl.BlockSpec((group, 3, chunk, cols), lambda g: (g, 0, 0, 0)),
    )(queries, keys, values)


def attend(blocks, flags, qkv, before, prior):
    peers, _, chunk, width = qkv.shape
    per_block = BLOCK // chunk
    rows = len(blocks) * per_block
    reads = (blocks[-1] + 1) * per_block if blocks[0] == 0 else peers
    operands = [flags, qkv]
    in_specs = [
        pl.BlockSpec(memory_space=pltpu.SMEM),
        pl.BlockSpec((reads,) + qkv.shape[1:3] + (HDIM,), lambda h: (0, 0, 0, h)),
    ]
    if before is not None:
        operands.append(before)
        in_specs.append(pl.BlockSpec(before.shape[:3] + (HDIM,), lambda h: (0, 0, 0, h)))
    aliases = {}
    if prior is not None:
        aliases = {len(operands): 0}
        operands.append(prior)
        in_specs.append(pl.BlockSpec(memory_space=pl.ANY))
    return pl.pallas_call(
        functools.partial(attention_kernel, blocks, before is not None),
        out_shape=jax.ShapeDtypeStruct((peers, chunk, width), qkv.dtype),
        grid=(width // HDIM,),
        in_specs=in_specs,
        out_specs=pl.BlockSpec((rows, chunk, HDIM), lambda h: (blocks[0] * per_block // rows, 0, h)),
        input_output_aliases=aliases,
    )(*operands)


def body(queries, keys, values, block_lists, block_counts):
    peers = lax.axis_size("head")
    chunk, width = queries.shape
    cols = width // peers
    per_block = BLOCK // chunk
    owned_blocks = peers // per_block
    reach = CYCLE - 1
    qkv_out = slabs(queries, keys, values, peers)
    qkv = lax.all_to_all(qkv_out, "head", split_axis=0, concat_axis=0, tiled=True)
    before = from_behind(qkv[peers - reach * per_block :, 1:], "blk", 1)
    own = lax.axis_index("blk")
    target = own * owned_blocks + jnp.arange(owned_blocks, dtype=jnp.int32)
    distance = reach - jnp.arange(CYCLE, dtype=jnp.int32)
    used = jnp.arange(CYCLE, dtype=jnp.int32)[None, :] < block_counts[:, None]
    hits = used[:, None, :] & (block_lists[:, None, :] == (target[:, None] - distance[None, :])[:, :, None])
    flags = jnp.any(hits, axis=2).astype(jnp.int32)
    late = tuple(range(min(reach, owned_blocks)))
    early = tuple(range(len(late), owned_blocks))
    joined = attend(early, flags, qkv, None, None) if early else None
    joined = attend(late, flags, qkv, before, joined)
    back = lax.all_to_all(joined, "head", split_axis=0, concat_axis=0, tiled=True)
    return back.transpose(1, 0, 2).reshape(chunk, width)


def solution(mesh):
    return jax.shard_map(
        body,
        mesh=mesh,
        in_specs=(
            P(("blk", "head"), None),
            P(("blk", "head"), None),
            P(("blk", "head"), None),
            P("blk", None),
            P("blk"),
        ),
        out_specs=P(("blk", "head"), None),
        check_vma=False,
    )
```

```python
import functools

import jax
import jax.numpy as jnp
from jax import lax
from jax.experimental import pallas as pl
from jax.experimental.pallas import tpu as pltpu
from jax.sharding import PartitionSpec as P

HEADS = 32
HDIM = 128
BLOCK = 256
CYCLE = 3
LOG2E = 1.4426950408889634


def from_behind(value, axis, steps):
    count = lax.axis_size(axis)
    initial, last = (max(0, -steps), min(count, count - steps))
    return lax.ppermute(value, axis, [(source, source + steps) for source in range(initial, last)])


def attention_kernel(blocks, has_before, flags_ref, qkv_ref, *refs):
    before_ref = refs[0] if has_before else None
    out_ref = refs[-1]
    _, _, chunk, width = qkv_ref.shape
    per_block = BLOCK // chunk
    out_first = blocks[0] * per_block
    local_heads = width // HDIM
    reach = CYCLE - 1
    scale = 1.0 / HDIM**0.5
    row_pos = lax.broadcasted_iota(jnp.int32, (BLOCK, CYCLE * BLOCK), 0)
    col_pos = lax.broadcasted_iota(jnp.int32, (BLOCK, CYCLE * BLOCK), 1)
    causal = (col_pos < reach * BLOCK) | (col_pos - reach * BLOCK <= row_pos)
    for local in blocks:
        allowed = causal
        for place in range(CYCLE):
            inside = (col_pos >= place * BLOCK) & (col_pos < (place + 1) * BLOCK)
            allowed = allowed & (jnp.logical_not(inside) | (flags_ref[local, place] != 0))
        rows = slice(local * per_block, (local + 1) * per_block)
        first = local - reach
        for head in range(local_heads):
            cols = slice(head * HDIM, (head + 1) * HDIM)
            q = qkv_ref[rows, 0, :, cols].reshape(BLOCK, HDIM)
            if first >= 0:
                span = slice(first * per_block, (local + 1) * per_block)
                k = qkv_ref[span, 1, :, cols].reshape(CYCLE * BLOCK, HDIM)
                v = qkv_ref[span, 2, :, cols].reshape(CYCLE * BLOCK, HDIM)
            else:
                halo = slice((first + reach) * per_block, reach * per_block)
                own = slice(0, (local + 1) * per_block)
                k = jnp.concatenate(
                    (before_ref[halo, 0, :, cols].reshape(-1, HDIM), qkv_ref[own, 1, :, cols].reshape(-1, HDIM)), axis=0
                )
                v = jnp.concatenate(
                    (before_ref[halo, 1, :, cols].reshape(-1, HDIM), qkv_ref[own, 2, :, cols].reshape(-1, HDIM)), axis=0
                )
            s = lax.dot_general(q, k, (((1,), (1,)), ((), ())), preferred_element_type=jnp.float32)
            s = jnp.where(allowed, s, -1e30)
            top = jnp.max(s, axis=1, keepdims=True)
            w = jnp.exp2((s - top) * (scale * LOG2E))
            total = jnp.sum(w, axis=1, keepdims=True)
            summed = jnp.dot(w.astype(jnp.bfloat16), v, preferred_element_type=jnp.float32)
            result = (summed / total).astype(out_ref.dtype)
            out_rows = slice(local * per_block - out_first, (local + 1) * per_block - out_first)
            out_ref[out_rows, :, cols] = result.reshape(per_block, chunk, HDIM)


def slab_kernel(q_hbm, k_hbm, v_hbm, out_hbm, sems):
    peers, _, _, cols = out_hbm.shape
    copies = []
    for t, ref in enumerate((q_hbm, k_hbm, v_hbm)):
        for dest in range(peers):
            copy = pltpu.make_async_copy(ref.at[:, pl.ds(dest * cols, cols)], out_hbm.at[dest, t], sems.at[t, dest])
            copy.start()
            copies.append(copy)
    for copy in copies:
        copy.wait()


def attend(blocks, flags, qkv, before, prior):
    peers, _, chunk, width = qkv.shape
    per_block = BLOCK // chunk
    rows = len(blocks) * per_block
    reads = (blocks[-1] + 1) * per_block if blocks[0] == 0 else peers
    operands = [flags, qkv]
    in_specs = [
        pl.BlockSpec(memory_space=pltpu.SMEM),
        pl.BlockSpec((reads,) + qkv.shape[1:], lambda i: (0, 0, 0, 0)),
    ]
    if before is not None:
        operands.append(before)
        in_specs.append(pl.BlockSpec(before.shape, lambda i: (0, 0, 0, 0)))
    aliases = {}
    if prior is not None:
        aliases = {len(operands): 0}
        operands.append(prior)
        in_specs.append(pl.BlockSpec(memory_space=pl.ANY))
    return pl.pallas_call(
        functools.partial(attention_kernel, blocks, before is not None),
        out_shape=jax.ShapeDtypeStruct((peers, chunk, width), qkv.dtype),
        grid=(1,),
        in_specs=in_specs,
        out_specs=pl.BlockSpec((rows, chunk, width), lambda i: (blocks[0] * per_block // rows, 0, 0)),
        input_output_aliases=aliases,
    )(*operands)


def body(queries, keys, values, block_lists, block_counts):
    peers = lax.axis_size("head")
    chunk, width = queries.shape
    cols = width // peers
    per_block = BLOCK // chunk
    owned_blocks = peers // per_block
    reach = CYCLE - 1
    anywhere = pl.BlockSpec(memory_space=pl.ANY)
    qkv_out = pl.pallas_call(
        slab_kernel,
        out_shape=jax.ShapeDtypeStruct((peers, 3, chunk, cols), queries.dtype),
        in_specs=[anywhere] * 3,
        out_specs=anywhere,
        scratch_shapes=[pltpu.SemaphoreType.DMA((3, peers))],
    )(queries, keys, values)
    qkv = lax.all_to_all(qkv_out, "head", split_axis=0, concat_axis=0, tiled=True)
    before = from_behind(qkv[peers - reach * per_block :, 1:], "blk", 1)
    own = lax.axis_index("blk")
    target = own * owned_blocks + jnp.arange(owned_blocks, dtype=jnp.int32)
    distance = reach - jnp.arange(CYCLE, dtype=jnp.int32)
    used = jnp.arange(CYCLE, dtype=jnp.int32)[None, :] < block_counts[:, None]
    hits = used[:, None, :] & (block_lists[:, None, :] == (target[:, None] - distance[None, :])[:, :, None])
    flags = jnp.any(hits, axis=2).astype(jnp.int32)
    late = tuple(range(min(reach, owned_blocks)))
    early = tuple(range(len(late), owned_blocks))
    joined = attend(early, flags, qkv, None, None) if early else None
    joined = attend(late, flags, qkv, before, joined)
    back = lax.all_to_all(joined, "head", split_axis=0, concat_axis=0, tiled=True)
    return back.transpose(1, 0, 2).reshape(chunk, width)


def solution(mesh):
    return jax.shard_map(
        body,
        mesh=mesh,
        in_specs=(
            P(("blk", "head"), None),
            P(("blk", "head"), None),
            P(("blk", "head"), None),
            P("blk", None),
            P("blk"),
        ),
        out_specs=P(("blk", "head"), None),
        check_vma=False,
    )
```

```python
import functools

import jax
import jax.numpy as jnp
from jax import lax
from jax.experimental import pallas as pl
from jax.experimental.pallas import tpu as pltpu
from jax.sharding import PartitionSpec as P

HEADS = 32
HDIM = 128
BLOCK = 256
CYCLE = 3
LOG2E = 1.4426950408889634


def from_behind(value, axis, steps):
    count = lax.axis_size(axis)
    initial, last = (max(0, -steps), min(count, count - steps))
    return lax.ppermute(value, axis, [(source, source + steps) for source in range(initial, last)])


def attention_kernel(blocks, has_before, flags_ref, qkv_ref, *refs):
    before_ref = refs[0] if has_before else None
    out_ref = refs[-1]
    _, _, chunk, width = qkv_ref.shape
    per_block = BLOCK // chunk
    out_first = blocks[0] * per_block
    local_heads = width // HDIM
    reach = CYCLE - 1
    scale = 1.0 / HDIM**0.5
    row_pos = lax.broadcasted_iota(jnp.int32, (BLOCK, CYCLE * BLOCK), 0)
    col_pos = lax.broadcasted_iota(jnp.int32, (BLOCK, CYCLE * BLOCK), 1)
    causal = (col_pos < reach * BLOCK) | (col_pos - reach * BLOCK <= row_pos)
    for local in blocks:
        allowed = causal
        for place in range(CYCLE):
            inside = (col_pos >= place * BLOCK) & (col_pos < (place + 1) * BLOCK)
            allowed = allowed & (jnp.logical_not(inside) | (flags_ref[local, place] != 0))
        rows = slice(local * per_block, (local + 1) * per_block)
        first = local - reach
        for head in range(local_heads):
            cols = slice(head * HDIM, (head + 1) * HDIM)
            q = qkv_ref[rows, 0, :, cols].reshape(BLOCK, HDIM)
            if first >= 0:
                span = slice(first * per_block, (local + 1) * per_block)
                k = qkv_ref[span, 1, :, cols].reshape(CYCLE * BLOCK, HDIM)
                v = qkv_ref[span, 2, :, cols].reshape(CYCLE * BLOCK, HDIM)
            else:
                halo = slice((first + reach) * per_block, reach * per_block)
                own = slice(0, (local + 1) * per_block)
                k = jnp.concatenate(
                    (before_ref[halo, 0, :, cols].reshape(-1, HDIM), qkv_ref[own, 1, :, cols].reshape(-1, HDIM)), axis=0
                )
                v = jnp.concatenate(
                    (before_ref[halo, 1, :, cols].reshape(-1, HDIM), qkv_ref[own, 2, :, cols].reshape(-1, HDIM)), axis=0
                )
            s = lax.dot_general(q, k, (((1,), (1,)), ((), ())), preferred_element_type=jnp.float32)
            s = jnp.where(allowed, s, -1e30)
            top = jnp.max(s, axis=1, keepdims=True)
            w = jnp.exp2((s - top) * (scale * LOG2E))
            total = jnp.sum(w, axis=1, keepdims=True)
            summed = jnp.dot(w.astype(jnp.bfloat16), v, preferred_element_type=jnp.float32)
            result = (summed / total).astype(out_ref.dtype)
            out_rows = slice(local * per_block - out_first, (local + 1) * per_block - out_first)
            out_ref[out_rows, :, cols] = result.reshape(per_block, chunk, HDIM)


def slab_kernel(q_ref, k_ref, v_ref, out_ref):
    peers, _, _, cols = out_ref.shape
    for t, ref in enumerate((q_ref, k_ref, v_ref)):
        for dest in range(peers):
            out_ref[dest, t] = ref[:, dest * cols : (dest + 1) * cols]


def attend(blocks, flags, qkv, before, prior):
    peers, _, chunk, width = qkv.shape
    per_block = BLOCK // chunk
    rows = len(blocks) * per_block
    reads = (blocks[-1] + 1) * per_block if blocks[0] == 0 else peers
    operands = [flags, qkv]
    in_specs = [
        pl.BlockSpec(memory_space=pltpu.SMEM),
        pl.BlockSpec((reads,) + qkv.shape[1:], lambda i: (0, 0, 0, 0)),
    ]
    if before is not None:
        operands.append(before)
        in_specs.append(pl.BlockSpec(before.shape, lambda i: (0, 0, 0, 0)))
    aliases = {}
    if prior is not None:
        aliases = {len(operands): 0}
        operands.append(prior)
        in_specs.append(pl.BlockSpec(memory_space=pl.ANY))
    return pl.pallas_call(
        functools.partial(attention_kernel, blocks, before is not None),
        out_shape=jax.ShapeDtypeStruct((peers, chunk, width), qkv.dtype),
        grid=(1,),
        in_specs=in_specs,
        out_specs=pl.BlockSpec((rows, chunk, width), lambda i: (blocks[0] * per_block // rows, 0, 0)),
        input_output_aliases=aliases,
    )(*operands)


def body(queries, keys, values, block_lists, block_counts):
    peers = lax.axis_size("head")
    chunk, width = queries.shape
    cols = width // peers
    per_block = BLOCK // chunk
    owned_blocks = peers // per_block
    reach = CYCLE - 1
    qkv_out = pl.pallas_call(
        slab_kernel,
        out_shape=jax.ShapeDtypeStruct((peers, 3, chunk, cols), queries.dtype),
        in_specs=[pl.BlockSpec(memory_space=pltpu.VMEM)] * 3,
        out_specs=pl.BlockSpec(memory_space=pltpu.VMEM),
    )(queries, keys, values)
    qkv = lax.all_to_all(qkv_out, "head", split_axis=0, concat_axis=0, tiled=True)
    before = from_behind(qkv[peers - reach * per_block :, 1:], "blk", 1)
    own = lax.axis_index("blk")
    target = own * owned_blocks + jnp.arange(owned_blocks, dtype=jnp.int32)
    distance = reach - jnp.arange(CYCLE, dtype=jnp.int32)
    used = jnp.arange(CYCLE, dtype=jnp.int32)[None, :] < block_counts[:, None]
    hits = used[:, None, :] & (block_lists[:, None, :] == (target[:, None] - distance[None, :])[:, :, None])
    flags = jnp.any(hits, axis=2).astype(jnp.int32)
    late = tuple(range(min(reach, owned_blocks)))
    early = tuple(range(len(late), owned_blocks))
    joined = attend(early, flags, qkv, None, None) if early else None
    joined = attend(late, flags, qkv, before, joined)
    back = lax.all_to_all(joined, "head", split_axis=0, concat_axis=0, tiled=True)
    return back.transpose(1, 0, 2).reshape(chunk, width)


def solution(mesh):
    return jax.shard_map(
        body,
        mesh=mesh,
        in_specs=(
            P(("blk", "head"), None),
            P(("blk", "head"), None),
            P(("blk", "head"), None),
            P("blk", None),
            P("blk"),
        ),
        out_specs=P(("blk", "head"), None),
        check_vma=False,
    )
```

```python
import functools

import jax
import jax.numpy as jnp
from jax import lax
from jax.experimental import pallas as pl
from jax.experimental.pallas import tpu as pltpu
from jax.sharding import PartitionSpec as P

HEADS = 32
HDIM = 128
BLOCK = 256
CYCLE = 3


def from_behind(value, axis, steps):
    count = lax.axis_size(axis)
    initial, last = (max(0, -steps), min(count, count - steps))
    return lax.ppermute(value, axis, [(source, source + steps) for source in range(initial, last)])


def attention_kernel(blocks, has_before, flags_ref, qkv_ref, *refs):
    before_ref = refs[0] if has_before else None
    out_ref = refs[-1]
    _, _, chunk, width = qkv_ref.shape
    per_block = BLOCK // chunk
    out_first = blocks[0] * per_block
    local_heads = width // HDIM
    reach = CYCLE - 1
    scale = 1.0 / HDIM**0.5
    row_pos = lax.broadcasted_iota(jnp.int32, (BLOCK, CYCLE * BLOCK), 0)
    col_pos = lax.broadcasted_iota(jnp.int32, (BLOCK, CYCLE * BLOCK), 1)
    causal = (col_pos < reach * BLOCK) | (col_pos - reach * BLOCK <= row_pos)
    for local in blocks:
        allowed = causal
        for place in range(CYCLE):
            inside = (col_pos >= place * BLOCK) & (col_pos < (place + 1) * BLOCK)
            allowed = allowed & (jnp.logical_not(inside) | (flags_ref[local, place] != 0))
        rows = slice(local * per_block, (local + 1) * per_block)
        first = local - reach
        for head in range(local_heads):
            cols = slice(head * HDIM, (head + 1) * HDIM)
            q = qkv_ref[rows, 0, :, cols].reshape(BLOCK, HDIM)
            if first >= 0:
                span = slice(first * per_block, (local + 1) * per_block)
                k = qkv_ref[span, 1, :, cols].reshape(CYCLE * BLOCK, HDIM)
                v = qkv_ref[span, 2, :, cols].reshape(CYCLE * BLOCK, HDIM)
            else:
                halo = slice((first + reach) * per_block, reach * per_block)
                own = slice(0, (local + 1) * per_block)
                k = jnp.concatenate(
                    (before_ref[halo, 0, :, cols].reshape(-1, HDIM), qkv_ref[own, 1, :, cols].reshape(-1, HDIM)), axis=0
                )
                v = jnp.concatenate(
                    (before_ref[halo, 1, :, cols].reshape(-1, HDIM), qkv_ref[own, 2, :, cols].reshape(-1, HDIM)), axis=0
                )
            s = lax.dot_general(q, k, (((1,), (1,)), ((), ())), preferred_element_type=jnp.float32) * scale
            s = jnp.where(allowed, s, -1e30)
            top = jnp.max(s, axis=1, keepdims=True)
            w = jnp.exp(s - top)
            total = jnp.sum(w, axis=1, keepdims=True)
            summed = jnp.dot(w.astype(jnp.bfloat16), v, preferred_element_type=jnp.float32)
            result = (summed / total).astype(out_ref.dtype)
            out_rows = slice(local * per_block - out_first, (local + 1) * per_block - out_first)
            out_ref[out_rows, :, cols] = result.reshape(per_block, chunk, HDIM)


def slab_kernel(q_ref, k_ref, v_ref, out_ref):
    peers, _, _, cols = out_ref.shape
    for t, ref in enumerate((q_ref, k_ref, v_ref)):
        for dest in range(peers):
            out_ref[dest, t] = ref[:, dest * cols : (dest + 1) * cols]


def attend(blocks, flags, qkv, before, prior):
    peers, _, chunk, width = qkv.shape
    per_block = BLOCK // chunk
    rows = len(blocks) * per_block
    reads = (blocks[-1] + 1) * per_block if blocks[0] == 0 else peers
    operands = [flags, qkv]
    in_specs = [
        pl.BlockSpec(memory_space=pltpu.SMEM),
        pl.BlockSpec((reads,) + qkv.shape[1:], lambda i: (0, 0, 0, 0)),
    ]
    if before is not None:
        operands.append(before)
        in_specs.append(pl.BlockSpec(before.shape, lambda i: (0, 0, 0, 0)))
    aliases = {}
    if prior is not None:
        aliases = {len(operands): 0}
        operands.append(prior)
        in_specs.append(pl.BlockSpec(memory_space=pl.ANY))
    return pl.pallas_call(
        functools.partial(attention_kernel, blocks, before is not None),
        out_shape=jax.ShapeDtypeStruct((peers, chunk, width), qkv.dtype),
        grid=(1,),
        in_specs=in_specs,
        out_specs=pl.BlockSpec((rows, chunk, width), lambda i: (blocks[0] * per_block // rows, 0, 0)),
        input_output_aliases=aliases,
    )(*operands)


def body(queries, keys, values, block_lists, block_counts):
    peers = lax.axis_size("head")
    chunk, width = queries.shape
    cols = width // peers
    per_block = BLOCK // chunk
    owned_blocks = peers // per_block
    reach = CYCLE - 1
    qkv_out = pl.pallas_call(
        slab_kernel,
        out_shape=jax.ShapeDtypeStruct((peers, 3, chunk, cols), queries.dtype),
        in_specs=[pl.BlockSpec(memory_space=pltpu.VMEM)] * 3,
        out_specs=pl.BlockSpec(memory_space=pltpu.VMEM),
    )(queries, keys, values)
    qkv = lax.all_to_all(qkv_out, "head", split_axis=0, concat_axis=0, tiled=True)
    before = from_behind(qkv[peers - reach * per_block :, 1:], "blk", 1)
    own = lax.axis_index("blk")
    target = own * owned_blocks + jnp.arange(owned_blocks, dtype=jnp.int32)
    distance = reach - jnp.arange(CYCLE, dtype=jnp.int32)
    used = jnp.arange(CYCLE, dtype=jnp.int32)[None, :] < block_counts[:, None]
    hits = used[:, None, :] & (block_lists[:, None, :] == (target[:, None] - distance[None, :])[:, :, None])
    flags = jnp.any(hits, axis=2).astype(jnp.int32)
    joined = attend(tuple(range(owned_blocks)), flags, qkv, before, None)
    back = lax.all_to_all(joined, "head", split_axis=0, concat_axis=0, tiled=True)
    return back.transpose(1, 0, 2).reshape(chunk, width)


def solution(mesh):
    return jax.shard_map(
        body,
        mesh=mesh,
        in_specs=(
            P(("blk", "head"), None),
            P(("blk", "head"), None),
            P(("blk", "head"), None),
            P("blk", None),
            P("blk"),
        ),
        out_specs=P(("blk", "head"), None),
        check_vma=False,
    )
```

```python
import functools

import jax
import jax.numpy as jnp
from jax import lax
from jax.experimental import pallas as pl
from jax.experimental.pallas import tpu as pltpu
from jax.sharding import PartitionSpec as P

HEADS = 32
HDIM = 128
BLOCK = 256
CYCLE = 3


def from_behind(value, axis, steps):
    count = lax.axis_size(axis)
    initial, last = (max(0, -steps), min(count, count - steps))
    return lax.ppermute(value, axis, [(source, source + steps) for source in range(initial, last)])


def attention_kernel(blocks, has_before, lists_ref, counts_ref, qkv_ref, *refs):
    before_ref = refs[0] if has_before else None
    out_ref = refs[-1]
    _, _, chunk, width = qkv_ref.shape
    per_block = BLOCK // chunk
    out_first = blocks[0] * per_block
    local_heads = width // HDIM
    reach = CYCLE - 1
    scale = 1.0 / HDIM**0.5
    row_pos = lax.broadcasted_iota(jnp.int32, (BLOCK, CYCLE * BLOCK), 0)
    col_pos = lax.broadcasted_iota(jnp.int32, (BLOCK, CYCLE * BLOCK), 1)
    causal = (col_pos < reach * BLOCK) | (col_pos - reach * BLOCK <= row_pos)
    owned_blocks = counts_ref.shape[0]
    target = lax.axis_index("blk").astype(jnp.int32) * owned_blocks
    for local in blocks:
        allowed = causal
        for place in range(CYCLE):
            inside = (col_pos >= place * BLOCK) & (col_pos < (place + 1) * BLOCK)
            wanted = None
            for entry in range(CYCLE):
                hit = (counts_ref[local] > entry) & (lists_ref[local, entry] == target + local - (reach - place))
                wanted = hit if wanted is None else wanted | hit
            allowed = allowed & (jnp.logical_not(inside) | wanted)
        rows = slice(local * per_block, (local + 1) * per_block)
        first = local - reach
        for head in range(local_heads):
            cols = slice(head * HDIM, (head + 1) * HDIM)
            q = qkv_ref[rows, 0, :, cols].reshape(BLOCK, HDIM)
            if first >= 0:
                span = slice(first * per_block, (local + 1) * per_block)
                k = qkv_ref[span, 1, :, cols].reshape(CYCLE * BLOCK, HDIM)
                v = qkv_ref[span, 2, :, cols].reshape(CYCLE * BLOCK, HDIM)
            else:
                halo = slice((first + reach) * per_block, reach * per_block)
                own = slice(0, (local + 1) * per_block)
                k = jnp.concatenate(
                    (before_ref[halo, 0, :, cols].reshape(-1, HDIM), qkv_ref[own, 1, :, cols].reshape(-1, HDIM)), axis=0
                )
                v = jnp.concatenate(
                    (before_ref[halo, 1, :, cols].reshape(-1, HDIM), qkv_ref[own, 2, :, cols].reshape(-1, HDIM)), axis=0
                )
            s = lax.dot_general(q, k, (((1,), (1,)), ((), ())), preferred_element_type=jnp.float32) * scale
            s = jnp.where(allowed, s, -1e30)
            top = jnp.max(s, axis=1, keepdims=True)
            w = jnp.exp(s - top)
            total = jnp.sum(w, axis=1, keepdims=True)
            summed = jnp.dot(w.astype(jnp.bfloat16), v, preferred_element_type=jnp.float32)
            result = (summed / total).astype(out_ref.dtype)
            out_rows = slice(local * per_block - out_first, (local + 1) * per_block - out_first)
            out_ref[out_rows, :, cols] = result.reshape(per_block, chunk, HDIM)


def slab_kernel(q_ref, k_ref, v_ref, out_ref):
    peers, _, _, cols = out_ref.shape
    for t, ref in enumerate((q_ref, k_ref, v_ref)):
        for dest in range(peers):
            out_ref[dest, t] = ref[:, dest * cols : (dest + 1) * cols]


def attend(blocks, block_lists, block_counts, qkv, before, prior):
    peers, _, chunk, width = qkv.shape
    per_block = BLOCK // chunk
    rows = len(blocks) * per_block
    reads = (blocks[-1] + 1) * per_block if blocks[0] == 0 else peers
    operands = [block_lists, block_counts, qkv]
    in_specs = [
        pl.BlockSpec(memory_space=pltpu.SMEM),
        pl.BlockSpec(memory_space=pltpu.SMEM),
        pl.BlockSpec((reads,) + qkv.shape[1:], lambda i: (0, 0, 0, 0)),
    ]
    if before is not None:
        operands.append(before)
        in_specs.append(pl.BlockSpec(before.shape, lambda i: (0, 0, 0, 0)))
    aliases = {}
    if prior is not None:
        aliases = {len(operands): 0}
        operands.append(prior)
        in_specs.append(pl.BlockSpec(memory_space=pl.ANY))
    return pl.pallas_call(
        functools.partial(attention_kernel, blocks, before is not None),
        out_shape=jax.ShapeDtypeStruct((peers, chunk, width), qkv.dtype),
        grid=(1,),
        in_specs=in_specs,
        out_specs=pl.BlockSpec((rows, chunk, width), lambda i: (blocks[0] * per_block // rows, 0, 0)),
        input_output_aliases=aliases,
    )(*operands)


def body(queries, keys, values, block_lists, block_counts):
    peers = lax.axis_size("head")
    chunk, width = queries.shape
    cols = width // peers
    per_block = BLOCK // chunk
    owned_blocks = peers // per_block
    reach = CYCLE - 1
    qkv_out = pl.pallas_call(
        slab_kernel,
        out_shape=jax.ShapeDtypeStruct((peers, 3, chunk, cols), queries.dtype),
        in_specs=[pl.BlockSpec(memory_space=pltpu.VMEM)] * 3,
        out_specs=pl.BlockSpec(memory_space=pltpu.VMEM),
    )(queries, keys, values)
    qkv = lax.all_to_all(qkv_out, "head", split_axis=0, concat_axis=0, tiled=True)
    before = from_behind(qkv[peers - reach * per_block :, 1:], "blk", 1)
    late = tuple(range(min(reach, owned_blocks)))
    early = tuple(range(len(late), owned_blocks))
    joined = attend(early, block_lists, block_counts, qkv, None, None) if early else None
    joined = attend(late, block_lists, block_counts, qkv, before, joined)
    back = lax.all_to_all(joined, "head", split_axis=0, concat_axis=0, tiled=True)
    return back.transpose(1, 0, 2).reshape(chunk, width)


def solution(mesh):
    return jax.shard_map(
        body,
        mesh=mesh,
        in_specs=(
            P(("blk", "head"), None),
            P(("blk", "head"), None),
            P(("blk", "head"), None),
            P("blk", None),
            P("blk"),
        ),
        out_specs=P(("blk", "head"), None),
        check_vma=False,
    )
```

```python
import functools

import jax
import jax.numpy as jnp
from jax import lax
from jax.experimental import pallas as pl
from jax.experimental.pallas import tpu as pltpu
from jax.sharding import PartitionSpec as P

HEADS = 32
HDIM = 128
BLOCK = 256
CYCLE = 3
LOG2E = 1.4426950408889634


def from_behind(value, axis, steps):
    count = lax.axis_size(axis)
    initial, last = (max(0, -steps), min(count, count - steps))
    return lax.ppermute(value, axis, [(source, source + steps) for source in range(initial, last)])


def attention_kernel(blocks, has_before, lists_ref, counts_ref, qkv_ref, *refs):
    before_ref = refs[0] if has_before else None
    out_ref = refs[-1]
    _, _, chunk, width = qkv_ref.shape
    per_block = BLOCK // chunk
    out_first = blocks[0] * per_block
    local_heads = width // HDIM
    reach = CYCLE - 1
    scale = 1.0 / HDIM**0.5
    row_pos = lax.broadcasted_iota(jnp.int32, (BLOCK, CYCLE * BLOCK), 0)
    col_pos = lax.broadcasted_iota(jnp.int32, (BLOCK, CYCLE * BLOCK), 1)
    causal = (col_pos < reach * BLOCK) | (col_pos - reach * BLOCK <= row_pos)
    owned_blocks = counts_ref.shape[0]
    target = lax.axis_index("blk").astype(jnp.int32) * owned_blocks
    for local in blocks:
        allowed = causal
        for place in range(CYCLE):
            inside = (col_pos >= place * BLOCK) & (col_pos < (place + 1) * BLOCK)
            wanted = None
            for entry in range(CYCLE):
                hit = (counts_ref[local] > entry) & (lists_ref[local, entry] == target + local - (reach - place))
                wanted = hit if wanted is None else wanted | hit
            allowed = allowed & (jnp.logical_not(inside) | wanted)
        rows = slice(local * per_block, (local + 1) * per_block)
        first = local - reach
        for head in range(local_heads):
            cols = slice(head * HDIM, (head + 1) * HDIM)
            q = qkv_ref[rows, 0, :, cols].reshape(BLOCK, HDIM)
            if first >= 0:
                span = slice(first * per_block, (local + 1) * per_block)
                k = qkv_ref[span, 1, :, cols].reshape(CYCLE * BLOCK, HDIM)
                v = qkv_ref[span, 2, :, cols].reshape(CYCLE * BLOCK, HDIM)
            else:
                halo = slice((first + reach) * per_block, reach * per_block)
                own = slice(0, (local + 1) * per_block)
                k = jnp.concatenate(
                    (before_ref[halo, 0, :, cols].reshape(-1, HDIM), qkv_ref[own, 1, :, cols].reshape(-1, HDIM)), axis=0
                )
                v = jnp.concatenate(
                    (before_ref[halo, 1, :, cols].reshape(-1, HDIM), qkv_ref[own, 2, :, cols].reshape(-1, HDIM)), axis=0
                )
            s = lax.dot_general(q, k, (((1,), (1,)), ((), ())), preferred_element_type=jnp.float32)
            s = jnp.where(allowed, s, -1e30)
            top = jnp.max(s, axis=1, keepdims=True)
            w = jnp.exp2((s - top) * (scale * LOG2E))
            total = jnp.sum(w, axis=1, keepdims=True)
            summed = jnp.dot(w.astype(jnp.bfloat16), v, preferred_element_type=jnp.float32)
            result = (summed / total).astype(out_ref.dtype)
            out_rows = slice(local * per_block - out_first, (local + 1) * per_block - out_first)
            out_ref[out_rows, :, cols] = result.reshape(per_block, chunk, HDIM)


def slab_kernel(q_ref, k_ref, v_ref, out_ref):
    peers, _, _, cols = out_ref.shape
    for t, ref in enumerate((q_ref, k_ref, v_ref)):
        for dest in range(peers):
            out_ref[dest, t] = ref[:, dest * cols : (dest + 1) * cols]


def attend(blocks, block_lists, block_counts, qkv, before, prior):
    peers, _, chunk, width = qkv.shape
    per_block = BLOCK // chunk
    rows = len(blocks) * per_block
    reads = (blocks[-1] + 1) * per_block if blocks[0] == 0 else peers
    operands = [block_lists, block_counts, qkv]
    in_specs = [
        pl.BlockSpec(memory_space=pltpu.SMEM),
        pl.BlockSpec(memory_space=pltpu.SMEM),
        pl.BlockSpec((reads,) + qkv.shape[1:], lambda i: (0, 0, 0, 0)),
    ]
    if before is not None:
        operands.append(before)
        in_specs.append(pl.BlockSpec(before.shape, lambda i: (0, 0, 0, 0)))
    aliases = {}
    if prior is not None:
        aliases = {len(operands): 0}
        operands.append(prior)
        in_specs.append(pl.BlockSpec(memory_space=pl.ANY))
    return pl.pallas_call(
        functools.partial(attention_kernel, blocks, before is not None),
        out_shape=jax.ShapeDtypeStruct((peers, chunk, width), qkv.dtype),
        grid=(1,),
        in_specs=in_specs,
        out_specs=pl.BlockSpec((rows, chunk, width), lambda i: (blocks[0] * per_block // rows, 0, 0)),
        input_output_aliases=aliases,
    )(*operands)


def body(queries, keys, values, block_lists, block_counts):
    peers = lax.axis_size("head")
    chunk, width = queries.shape
    cols = width // peers
    per_block = BLOCK // chunk
    owned_blocks = peers // per_block
    reach = CYCLE - 1
    qkv_out = pl.pallas_call(
        slab_kernel,
        out_shape=jax.ShapeDtypeStruct((peers, 3, chunk, cols), queries.dtype),
        in_specs=[pl.BlockSpec(memory_space=pltpu.VMEM)] * 3,
        out_specs=pl.BlockSpec(memory_space=pltpu.VMEM),
    )(queries, keys, values)
    qkv = lax.all_to_all(qkv_out, "head", split_axis=0, concat_axis=0, tiled=True)
    before = from_behind(qkv[peers - reach * per_block :, 1:], "blk", 1)
    late = tuple(range(min(reach, owned_blocks)))
    early = tuple(range(len(late), owned_blocks))
    joined = attend(early, block_lists, block_counts, qkv, None, None) if early else None
    joined = attend(late, block_lists, block_counts, qkv, before, joined)
    back = lax.all_to_all(joined, "head", split_axis=0, concat_axis=0, tiled=True)
    return back.transpose(1, 0, 2).reshape(chunk, width)


def solution(mesh):
    return jax.shard_map(
        body,
        mesh=mesh,
        in_specs=(
            P(("blk", "head"), None),
            P(("blk", "head"), None),
            P(("blk", "head"), None),
            P("blk", None),
            P("blk"),
        ),
        out_specs=P(("blk", "head"), None),
        check_vma=False,
    )
```

```python
import functools

import jax
import jax.numpy as jnp
from jax import lax
from jax.experimental import pallas as pl
from jax.experimental.pallas import tpu as pltpu
from jax.sharding import PartitionSpec as P

HEADS = 32
HDIM = 128
BLOCK = 256
CYCLE = 3
LOG2E = 1.4426950408889634


def from_behind(value, axis, steps):
    count = lax.axis_size(axis)
    initial, last = (max(0, -steps), min(count, count - steps))
    return lax.ppermute(value, axis, [(source, source + steps) for source in range(initial, last)])


def attention_kernel(blocks, has_before, lists_ref, counts_ref, qkv_ref, *refs):
    before_ref = refs[0] if has_before else None
    out_ref = refs[-1]
    _, _, chunk, width = qkv_ref.shape
    per_block = BLOCK // chunk
    out_first = blocks[0] * per_block
    local_heads = width // HDIM
    reach = CYCLE - 1
    scale = 1.0 / HDIM**0.5
    row_pos = lax.broadcasted_iota(jnp.int32, (BLOCK, CYCLE * BLOCK), 0)
    col_pos = lax.broadcasted_iota(jnp.int32, (BLOCK, CYCLE * BLOCK), 1)
    causal = (col_pos < reach * BLOCK) | (col_pos - reach * BLOCK <= row_pos)
    owned_blocks = counts_ref.shape[0]
    target = lax.axis_index("blk").astype(jnp.int32) * owned_blocks
    key_place = lax.broadcasted_iota(jnp.int32, (1, CYCLE * BLOCK), 1) // BLOCK
    for local in blocks:
        column_ok = None
        for place in range(CYCLE):
            wanted = None
            for entry in range(CYCLE):
                hit = (counts_ref[local] > entry) & (lists_ref[local, entry] == target + local - (reach - place))
                wanted = hit if wanted is None else wanted | hit
            here = (key_place == place) & wanted
            column_ok = here if column_ok is None else column_ok | here
        allowed = causal & column_ok
        rows = slice(local * per_block, (local + 1) * per_block)
        first = local - reach
        for head in range(local_heads):
            cols = slice(head * HDIM, (head + 1) * HDIM)
            q = qkv_ref[rows, 0, :, cols].reshape(BLOCK, HDIM)
            if first >= 0:
                span = slice(first * per_block, (local + 1) * per_block)
                k = qkv_ref[span, 1, :, cols].reshape(CYCLE * BLOCK, HDIM)
                v = qkv_ref[span, 2, :, cols].reshape(CYCLE * BLOCK, HDIM)
            else:
                halo = slice((first + reach) * per_block, reach * per_block)
                own = slice(0, (local + 1) * per_block)
                k = jnp.concatenate(
                    (before_ref[halo, 0, :, cols].reshape(-1, HDIM), qkv_ref[own, 1, :, cols].reshape(-1, HDIM)), axis=0
                )
                v = jnp.concatenate(
                    (before_ref[halo, 1, :, cols].reshape(-1, HDIM), qkv_ref[own, 2, :, cols].reshape(-1, HDIM)), axis=0
                )
            s = lax.dot_general(q, k, (((1,), (1,)), ((), ())), preferred_element_type=jnp.float32)
            s = jnp.where(allowed, s, -1e30)
            top = jnp.max(s, axis=1, keepdims=True)
            w = jnp.exp2((s - top) * (scale * LOG2E))
            total = jnp.sum(w, axis=1, keepdims=True)
            summed = jnp.dot(w.astype(jnp.bfloat16), v, preferred_element_type=jnp.float32)
            result = (summed / total).astype(out_ref.dtype)
            out_rows = slice(local * per_block - out_first, (local + 1) * per_block - out_first)
            out_ref[out_rows, :, cols] = result.reshape(per_block, chunk, HDIM)


def slab_kernel(q_ref, k_ref, v_ref, out_ref):
    peers, _, _, cols = out_ref.shape
    for t, ref in enumerate((q_ref, k_ref, v_ref)):
        for dest in range(peers):
            out_ref[dest, t] = ref[:, dest * cols : (dest + 1) * cols]


def attend(blocks, block_lists, block_counts, qkv, before, prior):
    peers, _, chunk, width = qkv.shape
    per_block = BLOCK // chunk
    rows = len(blocks) * per_block
    reads = (blocks[-1] + 1) * per_block if blocks[0] == 0 else peers
    operands = [block_lists, block_counts, qkv]
    in_specs = [
        pl.BlockSpec(memory_space=pltpu.SMEM),
        pl.BlockSpec(memory_space=pltpu.SMEM),
        pl.BlockSpec((reads,) + qkv.shape[1:], lambda i: (0, 0, 0, 0)),
    ]
    if before is not None:
        operands.append(before)
        in_specs.append(pl.BlockSpec(before.shape, lambda i: (0, 0, 0, 0)))
    aliases = {}
    if prior is not None:
        aliases = {len(operands): 0}
        operands.append(prior)
        in_specs.append(pl.BlockSpec(memory_space=pl.ANY))
    return pl.pallas_call(
        functools.partial(attention_kernel, blocks, before is not None),
        out_shape=jax.ShapeDtypeStruct((peers, chunk, width), qkv.dtype),
        grid=(1,),
        in_specs=in_specs,
        out_specs=pl.BlockSpec((rows, chunk, width), lambda i: (blocks[0] * per_block // rows, 0, 0)),
        input_output_aliases=aliases,
    )(*operands)


def body(queries, keys, values, block_lists, block_counts):
    peers = lax.axis_size("head")
    chunk, width = queries.shape
    cols = width // peers
    per_block = BLOCK // chunk
    owned_blocks = peers // per_block
    reach = CYCLE - 1
    qkv_out = pl.pallas_call(
        slab_kernel,
        out_shape=jax.ShapeDtypeStruct((peers, 3, chunk, cols), queries.dtype),
        in_specs=[pl.BlockSpec(memory_space=pltpu.VMEM)] * 3,
        out_specs=pl.BlockSpec(memory_space=pltpu.VMEM),
    )(queries, keys, values)
    qkv = lax.all_to_all(qkv_out, "head", split_axis=0, concat_axis=0, tiled=True)
    before = from_behind(qkv[peers - reach * per_block :, 1:], "blk", 1)
    late = tuple(range(min(reach, owned_blocks)))
    early = tuple(range(len(late), owned_blocks))
    joined = attend(early, block_lists, block_counts, qkv, None, None) if early else None
    joined = attend(late, block_lists, block_counts, qkv, before, joined)
    back = lax.all_to_all(joined, "head", split_axis=0, concat_axis=0, tiled=True)
    return back.transpose(1, 0, 2).reshape(chunk, width)


def solution(mesh):
    return jax.shard_map(
        body,
        mesh=mesh,
        in_specs=(
            P(("blk", "head"), None),
            P(("blk", "head"), None),
            P(("blk", "head"), None),
            P("blk", None),
            P("blk"),
        ),
        out_specs=P(("blk", "head"), None),
        check_vma=False,
    )
```
